1024 devices in a mesh: dp: 8 (over y), seq: 16 (over z), head: 8 (over x, core).
Axes of the slice: x: 4, y: 8, z: 16, core: 2. Of those that a mesh axis runs over, the one named last changes fastest.
Arguments:
- stream: bfloat16 [16384, 2048], P(('dp', 'seq')), parts along dimension 0, may hold values from -40 to 40
- queries: bfloat16 [16384, 2048], P(('dp', 'seq'), 'head'), parts along dimension 0, may hold values from -6 to 6
- keys: bfloat16 [16384, 2048], P(('dp', 'seq'), 'head'), parts along dimension 0, may hold values from -6 to 6
- values: bfloat16 [16384, 4096], P(('dp', 'seq'), 'head'), parts along dimension 0, may hold values from -6 to 6
- out_gate: bfloat16 [16384, 4096], P(('dp', 'seq'), 'head'), parts along dimension 0, may hold values from -6 to 6
- gates: float32 [16384, 32], P(('dp', 'seq'), 'head'), parts along dimension 0, may hold values from 0.25 to 1
- betas: float32 [16384, 32], P(('dp', 'seq'), 'head'), parts along dimension 0, may hold values from 0.01 to 0.08
- init_state: float32 [256, 128, 128], P(('dp', 'head')), parts along dimension 0, may hold values from -1.5 to 1.5
- norm_gain: float32 [128], replicated, may hold values from 0.5 to 1.5
- out_proj: bfloat16 [4096, 2048], P('head'), may hold values from -0.09375 to 0.09375
- post_gain: float32 [2048], replicated, may hold values from 0.5 to 1.5
- expert_ids: int32 [16384, 10], P(('dp', 'seq')), parts along dimension 0, may hold values from 0 to 127, all different within a row; in each aligned block of 128 rows (0 to 127, 128 to 255, ...) at most 20 rows name the same one
- route_scores: float32 [16384, 10], P(('dp', 'seq')), parts along dimension 0, may hold values from 0.05 to 1
- w_gate: bfloat16 [128, 2048, 512], P(('seq', 'head')), may hold values from -0.125 to 0.125
- w_up: bfloat16 [128, 2048, 512], P(('seq', 'head')), may hold values from -0.125 to 0.125
- w_down: bfloat16 [128, 512, 2048], P(('seq', 'head')), may hold values from -0.5 to 0.5
Outputs:
- layer_out: bfloat16 [16384, 2048], P(('dp', 'seq'), 'head'), parts along dimension 0
The draws below stay inside these ranges and needn't reach their ends.
There are 8 independent parts, one for each index of `dp`. The reference program is written for one: setup_inputs(seed, part) draws one part's arguments, and reference() takes and returns one part's arrays. A program takes and returns all parts, laid end to end along the dimension named above; an argument that names none is the same for every part. Nothing has to cross between parts.
Inputs may be any that keep to these rules, and one draw needn't show every extreme that they name: `expert_ids`: in each aligned block of 128 rows (the rows of one index of seq) no expert is named by more than 20 rows, a bound that some block reaches; the 10 experts of a row differ.
All inputs are finite; a program needn't handle non-finite values.
Results may differ from the reference program's by a relative error of at most 0.0095.
Values may be sent and summed in bfloat16 or wider, within the bound.
No kernel may reach another device: no remote copies, remote signals or barrier semaphores. Data moves between devices by JAX's collectives and lax.ppermute only.
A program may use at most 64 MiB of HBM per device.

```python
import math
import jax
import jax.numpy as jnp
import numpy as np
from jax import lax

D = 2048
VALUE_HEAD_COUNT = 32
QK_HEADS = 16
DK = 128
DV = 128
HID = 512
TOP = 10
TOK_DEV = 128
WINDOW_TOKENS = 2048
EXPERTS = 128
MOST = 20
N_SEQ = 16


def draw_gates(key, part):
    random_subkeys = jax.random.split(key, 6)
    fast_share = 0.5
    is_fast = jax.random.uniform(random_subkeys[0], (VALUE_HEAD_COUNT,)) < fast_share
    slow_rate = jax.random.uniform(random_subkeys[1], (VALUE_HEAD_COUNT,), minval=0.05, maxval=0.4) / WINDOW_TOKENS
    fast_rate = 1.0 / jax.random.uniform(random_subkeys[2], (VALUE_HEAD_COUNT,), minval=8.0, maxval=16.0)
    baseline_rate = jnp.where(is_fast, fast_rate, slow_rate)
    position = jnp.arange(WINDOW_TOKENS, dtype=jnp.float32)[:, None] / WINDOW_TOKENS
    phase_shift = jax.random.uniform(random_subkeys[3], (VALUE_HEAD_COUNT,), minval=0.0, maxval=6.28)
    variation_multiplier = jnp.exp2(jnp.sin(12.566371 * position + phase_shift[None, :]))
    coarse_multiplier = jax.random.uniform(random_subkeys[4], (WINDOW_TOKENS, VALUE_HEAD_COUNT), minval=0.5, maxval=2.0)
    spike_sample = jax.random.uniform(random_subkeys[5], (WINDOW_TOKENS, VALUE_HEAD_COUNT))
    spike_magnitude = jax.random.uniform(jax.random.fold_in(key, 7), (WINDOW_TOKENS, VALUE_HEAD_COUNT), minval=0.5, maxval=0.8)
    spike_logarithm = jnp.where(spike_sample < 2.0 / WINDOW_TOKENS, jnp.log(spike_magnitude), 0.0)
    return jnp.exp(spike_logarithm - baseline_rate[None, :] * variation_multiplier * coarse_multiplier).astype(jnp.float32)


def draw_stream(key, part):
    random_subkeys = jax.random.split(key, 3)
    base_vals = jax.random.truncated_normal(random_subkeys[0], -4.0, 4.0, (WINDOW_TOKENS, D))
    row_scale = jnp.exp(jax.random.uniform(random_subkeys[1], (WINDOW_TOKENS, 1), minval=-1.6, maxval=0.7))
    col_place = jnp.arange(D, dtype=jnp.float32)[None, :] / D
    col_scale = jnp.exp(1.0986 * col_place + jax.random.uniform(random_subkeys[2], (1, D), minval=-0.5, maxval=0.5))
    return (base_vals * row_scale * col_scale).astype(jnp.bfloat16)


def steps_of(rng, shape, pieces, least, top_value):
    def one(dim, blocks):
        heights = jax.random.uniform(jax.random.fold_in(jax.random.fold_in(rng, 6), dim), (blocks,), jnp.float32, least / len(pieces), top_value / len(pieces))
        return jnp.repeat(jnp.exp(heights), shape[dim] // blocks).reshape((-1,) + (1,) * (len(shape) - dim - 1))

    factor_of = one(*pieces[0])
    for cut in pieces[1:]:
        factor_of = factor_of * one(*cut)
    return factor_of


def assign_block(rng, own, number, rows, count, top, reach, slope):
    order = jax.random.permutation(rng, count)
    crowded, common = portions_of(count, rows * top, reach, slope, True), portions_of(count, rows * top, reach, slope, False)
    places = jnp.arange(count)

    def named(tallies, offset_by):
        used = int((tallies > 0).sum())
        fixed = max(1, used // 4)
        passed = fixed + (places - fixed + offset_by * (used - fixed)) % max(1, count - fixed)
        return jnp.zeros((count,), jnp.int32).at[order[jnp.where(places < fixed, places, passed)]].set(jnp.asarray(tallies, jnp.int32))

    tallies = jnp.where(number % 4 == 0, named(crowded, number // 4), named(common, number - number // 4 - 1))
    mixed = jax.random.permutation(jax.random.fold_in(own, 3), count)
    giver, sink = mixed[0:count // 2 * 2:2], mixed[1:count // 2 * 2:2]
    room = jnp.minimum(tallies[giver] - 1, reach - tallies[sink]) // 2
    room = jnp.where((giver == order[0]) | (sink == order[0]) | (tallies[sink] == 0), 0, jnp.maximum(room, 0))
    passed = jax.random.randint(jax.random.fold_in(own, 4), (count // 2,), 0, 1 << 20) % (room + 1)
    tallies = tallies.at[giver].add(-passed).at[sink].add(passed)
    items = jnp.searchsorted(jnp.cumsum(tallies), jnp.arange(rows * top), side="right").astype(jnp.int32)
    grid = items.reshape(top, rows).T
    grid = grid[jax.random.permutation(jax.random.fold_in(own, 1), rows)]
    offset_by = jax.random.randint(jax.random.fold_in(own, 2), (rows, 1), 0, top)
    return jnp.take_along_axis(grid, (jnp.arange(top)[None, :] + offset_by) % top, axis=1)


def portions_of(count, total, reach, slope, full):
    portions = [(1 << 20) // math.isqrt(standing ** slope) + 1 for standing in range(1, count + 1)]
    largest = reach if full else min(reach, max(-(-total // count), total * portions[0] // sum(portions)))
    least = 1 if total - largest >= count - 1 else 0
    given, spare = [largest] + [least] * (count - 1), total - largest - least * (count - 1)
    while spare > 0:
        free = [i for i in range(1, count) if given[i] < largest] or [i for i in range(1, count) if given[i] < reach]
        whole, budget = sum([portions[i] for i in free]), spare
        for i in free:
            addition = min(reach - given[i], max(1, budget * portions[i] // whole), spare)
            given[i] = given[i] + addition
            spare = spare - addition
    return np.array(given)


def gaussian(stream_key, extent, width, limit, cuts=(), held_as=jnp.bfloat16):
    values = jax.random.normal(stream_key, extent, jnp.float32) * width
    if len(cuts) > 0:
        values = steps_of(stream_key, extent, cuts, -0.22, 0.18) * values
    return jnp.clip(values, min=-limit, max=limit).astype(held_as)


def setup_inputs(seed: int = 0, part: int = 0) -> dict:
    arg_keys = jax.random.split(jax.random.key(seed), 17)
    part_splits = jax.random.split(jax.random.fold_in(arg_keys[16], part), 17)
    stream = draw_stream(jax.random.fold_in(jax.random.fold_in(arg_keys[16], part), 71), part)
    queries = gaussian(part_splits[1], (WINDOW_TOKENS, QK_HEADS * DK), 1.0, 6.0, ((0, 16), (1, 8)))
    keys = gaussian(part_splits[2], (WINDOW_TOKENS, QK_HEADS * DK), 1.0, 6.0, ((0, 16), (1, 8)))
    values = gaussian(part_splits[3], (WINDOW_TOKENS, VALUE_HEAD_COUNT * DV), 1.0, 6.0, ((0, 16), (1, 8)))
    out_gate = gaussian(part_splits[4], (WINDOW_TOKENS, VALUE_HEAD_COUNT * DV), 1.0, 6.0, ((0, 16), (1, 8)))
    gates = draw_gates(jax.random.fold_in(jax.random.fold_in(arg_keys[16], part), 71), part)
    betas = jnp.clip(0.01 + 0.07 * jax.random.uniform(part_splits[6], (WINDOW_TOKENS, VALUE_HEAD_COUNT), jnp.float32) ** steps_of(part_splits[6], (WINDOW_TOKENS, VALUE_HEAD_COUNT), ((0, 16), (1, 8)), -0.2, 0.2), 0.01, 0.08)
    init_state = gaussian(part_splits[7], (VALUE_HEAD_COUNT, DK, DV), 0.1, 1.5, ((0, 8),), jnp.float32)
    norm_gain = jnp.clip(1.0 + 0.1 * jax.random.normal(arg_keys[8], (DV,), jnp.float32), 0.5, 1.5)
    out_proj = gaussian(arg_keys[9], (VALUE_HEAD_COUNT * DV, D), (VALUE_HEAD_COUNT * DV) ** -0.5, 0.09375, ((0, 8),))
    post_gain = jnp.clip(1.0 + 0.1 * jax.random.normal(arg_keys[10], (D,), jnp.float32), 0.5, 1.5)
    expert_ids_keys = jax.random.split(jax.random.fold_in(part_splits[11], 1), WINDOW_TOKENS // TOK_DEV)
    expert_ids_turns = jax.random.permutation(jax.random.fold_in(part_splits[11], 3), WINDOW_TOKENS // TOK_DEV)
    expert_ids = jax.vmap(lambda own, number: assign_block(jax.random.fold_in(part_splits[11], 2), own, number, TOK_DEV, EXPERTS, TOP, MOST, 1))(expert_ids_keys, expert_ids_turns).reshape((WINDOW_TOKENS, TOP))
    route_scores = jnp.clip(jnp.exp(math.log(1.0) - 2.9957323 * jax.random.uniform(part_splits[12], (WINDOW_TOKENS, TOP), jnp.float32) ** steps_of(part_splits[12], (WINDOW_TOKENS, TOP), ((0, 16),), -0.2, 0.2)), 0.05, 1.0)
    w_gate = gaussian(arg_keys[13], (EXPERTS, D, HID), D ** -0.5, 0.125, ((0, 128),))
    w_up = gaussian(arg_keys[14], (EXPERTS, D, HID), D ** -0.5, 0.125, ((0, 128),))
    w_down = gaussian(arg_keys[15], (EXPERTS, HID, D), (HID // 4) ** -0.5, 0.5, ((0, 128),))
    return dict(stream=stream, queries=queries, keys=keys, values=values, out_gate=out_gate, gates=gates, betas=betas, init_state=init_state, norm_gain=norm_gain, out_proj=out_proj, post_gain=post_gain, expert_ids=expert_ids, route_scores=route_scores, w_gate=w_gate, w_up=w_up, w_down=w_down)


precise_variant = lax.Precision.HIGHEST

def unit_rows(matrix):
    return matrix * lax.rsqrt(lax.optimization_barrier(jnp.sum(matrix * matrix, axis=-1, keepdims=True)) + 1e-06)

def reference(stream, queries, keys, values, out_gate, gates, betas, init_state, norm_gain, out_proj, post_gain, expert_ids, route_scores, w_gate, w_up, w_down):
    tokens_all = stream.shape[0]
    group_size = VALUE_HEAD_COUNT // QK_HEADS
    scaled_q = unit_rows(queries.astype(jnp.float32).reshape(tokens_all, QK_HEADS, DK)) * DK ** (-0.5)
    scaled_q = jnp.repeat(scaled_q, group_size, axis=1)
    unit_k = jnp.repeat(unit_rows(keys.astype(jnp.float32).reshape(tokens_all, QK_HEADS, DK)), group_size, axis=1)
    value_rows = values.astype(jnp.float32).reshape(tokens_all, VALUE_HEAD_COUNT, DV)

    def advance(memory_state, inputs):
        query_at_step, key_at_step, value_t, gate_t, beta_t = inputs
        memory_state = memory_state * gate_t[:, None, None]
        retrieved_value = jnp.einsum('ne,nef->nf', key_at_step, memory_state, precision=precise_variant)
        delta = (value_t - retrieved_value) * beta_t[:, None]
        memory_state = memory_state + key_at_step[:, :, None] * delta[:, None, :]
        return (memory_state, jnp.einsum('ne,nef->nf', query_at_step, memory_state, precision=precise_variant))
    final_state, core = lax.scan(advance, init_state.astype(jnp.float32), (scaled_q, unit_k, value_rows, gates, betas))
    gate_rows = out_gate.astype(jnp.float32).reshape(tokens_all, VALUE_HEAD_COUNT, DV)
    gated = core * lax.rsqrt(lax.optimization_barrier(jnp.mean(core * core, axis=-1, keepdims=True)) + 1e-06) * norm_gain * jax.nn.silu(gate_rows)
    gated = gated.astype(jnp.bfloat16).reshape(tokens_all, VALUE_HEAD_COUNT * DV)
    attn = jnp.dot(gated, out_proj, preferred_element_type=jnp.float32)
    resid = (stream.astype(jnp.float32) + attn).astype(jnp.bfloat16)
    resid = lax.optimization_barrier(resid)
    resid_f = resid.astype(jnp.float32)
    normed = (resid_f * lax.rsqrt(lax.optimization_barrier(jnp.mean(resid_f * resid_f, axis=-1, keepdims=True)) + 1e-06) * post_gain).astype(jnp.bfloat16)
    weights = (route_scores / lax.optimization_barrier(jnp.sum(route_scores, axis=1, keepdims=True))).astype(jnp.bfloat16)
    weights = lax.optimization_barrier(weights).astype(jnp.float32)
    capacity = N_SEQ * MOST

    def expert_pass(mixed, expert):
        hits = expert_ids == expert
        chosen = jnp.any(hits, axis=1)
        token_w = lax.optimization_barrier(jnp.sum(jnp.where(hits, weights, 0.0), axis=1))
        picked = jnp.nonzero(chosen, size=capacity, fill_value=0)[0].astype(jnp.int32)
        valid = jnp.arange(capacity, dtype=jnp.int32) < jnp.sum(chosen.astype(jnp.int32))
        inputs_e = normed[picked]
        gate_e = jnp.dot(inputs_e, w_gate[expert], preferred_element_type=jnp.float32)
        up_e = jnp.dot(inputs_e, w_up[expert], preferred_element_type=jnp.float32)
        hidden = (jax.nn.silu(gate_e) * up_e).astype(jnp.bfloat16)
        result = jnp.dot(hidden, w_down[expert], preferred_element_type=jnp.float32).astype(jnp.bfloat16)
        result = lax.optimization_barrier(result).astype(jnp.float32)
        term = jnp.where(valid[:, None], token_w[picked][:, None] * result, 0.0)
        return (mixed.at[picked].add(term), None)
    moe, unused = lax.scan(expert_pass, jnp.zeros(stream.shape, jnp.float32), jnp.arange(EXPERTS, dtype=jnp.int32))
    return (resid_f + moe).astype(jnp.bfloat16)
```

```python
import jax
import jax.numpy as jnp
from jax import lax
from jax.sharding import PartitionSpec as P

VALUE_HEAD_COUNT = 32
QK_HEADS = 16
DK = 128
DV = 128


precise_variant = lax.Precision.HIGHEST


def unit_rows(matrix):
    return matrix * lax.rsqrt(jnp.sum(matrix * matrix, axis=-1, keepdims=True) + 1e-06)


def batch_product(left, right):
    return jnp.einsum("hij,hjk->hik", left, right, precision=precise_variant)


def on_device(
    stream,
    queries,
    keys,
    values,
    out_gate,
    gates,
    betas,
    init_state,
    norm_gain,
    out_proj,
    post_gain,
    expert_ids,
    route_scores,
    w_gate,
    w_up,
    w_down,
):
    length = stream.shape[0]
    model_width = stream.shape[1]
    head_count = values.shape[1] // DV
    group_size = VALUE_HEAD_COUNT // QK_HEADS
    scaled_q = unit_rows(queries.astype(jnp.float32).reshape(length, -1, DK)) * DK ** (-0.5)
    query_head_rows = jnp.repeat(scaled_q, group_size, axis=1).transpose(1, 0, 2)
    unit_k = unit_rows(keys.astype(jnp.float32).reshape(length, -1, DK))
    key_heads = jnp.repeat(unit_k, group_size, axis=1).transpose(1, 0, 2)
    value_heads = values.astype(jnp.float32).reshape(length, head_count, DV).transpose(1, 0, 2)
    beta_heads = betas.T
    log_decay = jnp.cumsum(jnp.log(gates), axis=0).T
    row_index = lax.broadcasted_iota(jnp.int32, (length, length), 0)
    col_index = lax.broadcasted_iota(jnp.int32, (length, length), 1)
    lower = row_index >= col_index
    strict = row_index > col_index
    gap_log = log_decay[:, :, None] - log_decay[:, None, :]
    decay = jnp.where(lower, jnp.exp(jnp.where(lower, gap_log, 0.0)), 0.0)
    key_inner = jnp.einsum("htk,hsk->hts", key_heads, key_heads, precision=precise_variant)
    tri_matrix = jnp.where(strict, decay * key_inner, 0.0) * beta_heads[:, :, None] + jnp.eye(
        length, dtype=jnp.float32
    )
    decay_factor = jnp.exp(log_decay)
    right_side = jnp.concatenate(
        [beta_heads[:, :, None] * value_heads, (beta_heads * decay_factor)[:, :, None] * key_heads],
        axis=-1,
    )
    solved = lax.linalg.triangular_solve(
        tri_matrix, right_side, left_side=True, lower=True, unit_diagonal=True
    )
    new_contribution = solved[:, :, :DV]
    carried_state = solved[:, :, DV:]
    tail_decay = jnp.exp(log_decay[:, -1:] - log_decay)
    keys_weighted = key_heads * tail_decay[:, :, None]
    eye_keys = jnp.eye(DK, dtype=jnp.float32)
    state_map = decay_factor[:, -1][:, None, None] * eye_keys - jnp.einsum(
        "htk,htj->hkj", keys_weighted, carried_state, precision=precise_variant
    )
    state_increment = jnp.einsum(
        "iys,iyn->isn", keys_weighted, new_contribution, precision=precise_variant
    )

    pairs = lax.all_gather(
        jnp.concatenate([state_map, state_increment], axis=0).astype(jnp.bfloat16), "seq"
    )

    def horner(k, state):
        step_pair = pairs[k].astype(jnp.float32)
        return batch_product(step_pair[:head_count], state) + step_pair[head_count:]

    opening_state = lax.fori_loop(0, lax.axis_index("seq"), horner, init_state)
    written_rows = new_contribution - jnp.einsum(
        "ucx,uxj->ucj", carried_state, opening_state, precision=precise_variant
    )
    query_inner = (
        jnp.einsum("htk,hsk->hts", query_head_rows, key_heads, precision=precise_variant) * decay
    )
    core = jnp.einsum(
        "ucx,uxj->ucj",
        query_head_rows * decay_factor[:, :, None],
        opening_state,
        precision=precise_variant,
    )
    core = core + jnp.einsum("hts,hsv->htv", query_inner, written_rows, precision=precise_variant)
    core = core.transpose(1, 0, 2)
    gate_rows = out_gate.astype(jnp.float32).reshape(length, head_count, DV)
    gated = (
        core
        * lax.rsqrt(jnp.mean(core * core, axis=-1, keepdims=True) + 1e-06)
        * norm_gain
        * jax.nn.silu(gate_rows)
    )
    gated = gated.astype(jnp.bfloat16).reshape(length, head_count * DV)
    attn_part = jnp.dot(gated, out_proj, preferred_element_type=jnp.float32)
    share_width = model_width // lax.axis_size("head")
    share_start = lax.axis_index("head") * share_width
    column_total = lax.axis_size("head")
    attn_pieces = attn_part.astype(jnp.bfloat16).reshape(length, column_total, share_width)
    attn_pieces = lax.all_to_all(
        attn_pieces.transpose(1, 0, 2), "head", split_axis=0, concat_axis=0, tiled=True
    )
    attn_share = jnp.sum(attn_pieces.astype(jnp.float32), axis=0)
    stream_share = lax.dynamic_slice_in_dim(stream, share_start, share_width, 1)
    resid_share = (stream_share.astype(jnp.float32) + attn_share).astype(jnp.bfloat16)
    resid_share = lax.optimization_barrier(resid_share)
    resid_rows = lax.all_to_all(
        jnp.broadcast_to(resid_share[None], (column_total, length, share_width)),
        "head",
        split_axis=0,
        concat_axis=0,
        tiled=True,
    )
    resid = resid_rows.transpose(1, 0, 2).reshape(length, model_width)
    resid_f = resid.astype(jnp.float32)
    normed = (
        resid_f * lax.rsqrt(jnp.mean(resid_f * resid_f, axis=-1, keepdims=True) + 1e-06) * post_gain
    ).astype(jnp.bfloat16)
    peer_count = lax.axis_size("seq")
    column_count = lax.axis_size("head")
    expert_count = peer_count * column_count
    pick_count = expert_ids.shape[1]
    slot_count = min(length, length * pick_count * 2 // expert_count)
    targets = jnp.arange(peer_count, dtype=jnp.int32) * column_count + lax.axis_index("head")
    hits = expert_ids[:, :, None] == targets[None, None, :]
    weights = (route_scores / jnp.sum(route_scores, axis=1, keepdims=True)).astype(jnp.bfloat16)
    weights = lax.optimization_barrier(weights).astype(jnp.float32)
    chosen = jnp.sum(hits.astype(jnp.int32), axis=1)
    share_weight = jnp.sum(jnp.where(hits, weights[:, :, None], 0.0), axis=1)
    rank = jnp.cumsum(chosen, axis=0) - chosen
    slot_index = jnp.arange(slot_count, dtype=jnp.int32)
    placement_map = (
        (chosen[:, :, None] == 1) & (rank[:, :, None] == slot_index[None, None, :])
    ).astype(jnp.bfloat16)
    outgoing = jnp.einsum(
        "tps,td->psd", placement_map, normed, preferred_element_type=jnp.float32
    ).astype(jnp.bfloat16)
    incoming = lax.all_to_all(outgoing, "seq", split_axis=0, concat_axis=0, tiled=True)
    item_count = incoming.shape[1]
    flat_rows = incoming.reshape(-1, model_width)
    gate_e = jnp.dot(flat_rows, w_gate[0], preferred_element_type=jnp.float32)
    up_e = jnp.dot(flat_rows, w_up[0], preferred_element_type=jnp.float32)
    hidden = (jax.nn.silu(gate_e) * up_e).astype(jnp.bfloat16)
    result = jnp.dot(hidden, w_down[0], preferred_element_type=jnp.float32).astype(jnp.bfloat16)
    returned = lax.all_to_all(
        result.reshape(peer_count, item_count, model_width),
        "seq",
        split_axis=0,
        concat_axis=0,
        tiled=True,
    )
    combine_map = (placement_map.astype(jnp.float32) * share_weight[:, :, None]).astype(
        jnp.bfloat16
    )
    moe = jnp.einsum("tps,psd->td", combine_map, returned, preferred_element_type=jnp.float32)
    moe_pieces = moe.astype(jnp.bfloat16).reshape(length, column_total, share_width)
    moe_pieces = lax.all_to_all(
        moe_pieces.transpose(1, 0, 2), "head", split_axis=0, concat_axis=0, tiled=True
    )
    moe_share = jnp.sum(moe_pieces.astype(jnp.float32), axis=0)
    return (resid_share.astype(jnp.float32) + moe_share).astype(jnp.bfloat16)


def solution(mesh):
    return jax.shard_map(
        on_device,
        mesh=mesh,
        in_specs=(
            P(("dp", "seq"), None),
            P(("dp", "seq"), "head"),
            P(("dp", "seq"), "head"),
            P(("dp", "seq"), "head"),
            P(("dp", "seq"), "head"),
            P(("dp", "seq"), "head"),
            P(("dp", "seq"), "head"),
            P(("dp", "head"), None, None),
            P(),
            P("head", None),
            P(),
            P(("dp", "seq"), None),
            P(("dp", "seq"), None),
            P(("seq", "head"), None, None),
            P(("seq", "head"), None, None),
            P(("seq", "head"), None, None),
        ),
        out_specs=P(("dp", "seq"), "head"),
        check_vma=False,
    )
```

```python
import jax
import jax.numpy as jnp
from jax import lax
from jax.sharding import PartitionSpec as P

VALUE_HEAD_COUNT = 32
QK_HEADS = 16
DK = 128
DV = 128


precise_variant = lax.Precision.HIGHEST


def unit_rows(matrix):
    return matrix * lax.rsqrt(jnp.sum(matrix * matrix, axis=-1, keepdims=True) + 1e-06)


def batch_product(left, right):
    return jnp.einsum("hij,hjk->hik", left, right, precision=precise_variant)


def block_product(left, right):
    return jnp.einsum("...ij,...jk->...ik", left, right, precision=precise_variant)


def unit_lower_inverse(tri, block=16):
    heads, size_all, _ = tri.shape
    count = size_all // block
    eye_block = jnp.eye(block, dtype=tri.dtype)
    diagonal = jnp.stack(
        [tri[:, k * block : (k + 1) * block, k * block : (k + 1) * block] for k in range(count)],
        axis=1,
    )
    nil = diagonal - eye_block
    power = block_product(nil, nil)
    inverse = block_product(eye_block - nil, eye_block + power)
    reach = 4
    while reach < block:
        power = block_product(power, power)
        inverse = block_product(inverse, eye_block + power)
        reach *= 2
    size = block
    while size < size_all:
        pairs = inverse.shape[1] // 2
        first = inverse[:, 0::2]
        second = inverse[:, 1::2]
        coupling = jnp.stack(
            [
                tri[:, (2 * k + 1) * size : (2 * k + 2) * size, 2 * k * size : (2 * k + 1) * size]
                for k in range(pairs)
            ],
            axis=1,
        )
        lower_left = -block_product(second, block_product(coupling, first))
        top = jnp.concatenate([first, jnp.zeros_like(first)], axis=-1)
        bottom = jnp.concatenate([lower_left, second], axis=-1)
        inverse = jnp.concatenate([top, bottom], axis=-2)
        size *= 2
    return inverse[:, 0]


def on_device(
    stream,
    queries,
    keys,
    values,
    out_gate,
    gates,
    betas,
    init_state,
    norm_gain,
    out_proj,
    post_gain,
    expert_ids,
    route_scores,
    w_gate,
    w_up,
    w_down,
):
    length = stream.shape[0]
    model_width = stream.shape[1]
    head_count = values.shape[1] // DV
    group_size = VALUE_HEAD_COUNT // QK_HEADS
    scaled_q = unit_rows(queries.astype(jnp.float32).reshape(length, -1, DK)) * DK ** (-0.5)
    query_head_rows = jnp.repeat(scaled_q, group_size, axis=1).transpose(1, 0, 2)
    unit_k = unit_rows(keys.astype(jnp.float32).reshape(length, -1, DK))
    key_heads = jnp.repeat(unit_k, group_size, axis=1).transpose(1, 0, 2)
    value_heads = values.astype(jnp.float32).reshape(length, head_count, DV).transpose(1, 0, 2)
    beta_heads = betas.T
    log_decay = jnp.cumsum(jnp.log(gates), axis=0).T
    row_index = lax.broadcasted_iota(jnp.int32, (length, length), 0)
    col_index = lax.broadcasted_iota(jnp.int32, (length, length), 1)
    lower = row_index >= col_index
    strict = row_index > col_index
    gap_log = log_decay[:, :, None] - log_decay[:, None, :]
    decay = jnp.where(lower, jnp.exp(jnp.where(lower, gap_log, 0.0)), 0.0)
    key_inner = jnp.einsum("htk,hsk->hts", key_heads, key_heads, precision=precise_variant)
    tri_matrix = jnp.where(strict, decay * key_inner, 0.0) * beta_heads[:, :, None] + jnp.eye(
        length, dtype=jnp.float32
    )
    decay_factor = jnp.exp(log_decay)
    right_side = jnp.concatenate(
        [beta_heads[:, :, None] * value_heads, (beta_heads * decay_factor)[:, :, None] * key_heads],
        axis=-1,
    )
    solved = batch_product(unit_lower_inverse(tri_matrix), right_side)
    new_contribution = solved[:, :, :DV]
    carried_state = solved[:, :, DV:]
    tail_decay = jnp.exp(log_decay[:, -1:] - log_decay)
    keys_weighted = key_heads * tail_decay[:, :, None]
    eye_keys = jnp.eye(DK, dtype=jnp.float32)
    state_map = decay_factor[:, -1][:, None, None] * eye_keys - jnp.einsum(
        "htk,htj->hkj", keys_weighted, carried_state, precision=precise_variant
    )
    state_increment = jnp.einsum(
        "iys,iyn->isn", keys_weighted, new_contribution, precision=precise_variant
    )

    query_inner = (
        jnp.einsum("htk,hsk->hts", query_head_rows, key_heads, precision=precise_variant) * decay
    )
    query_effective = query_head_rows * decay_factor[:, :, None] - batch_product(
        query_inner, carried_state
    )
    core_local = batch_product(query_inner, new_contribution)
    pairs = lax.all_gather(
        jnp.concatenate([state_map, state_increment], axis=0).astype(jnp.bfloat16), "seq"
    )
    segments = pairs.astype(jnp.float32)
    position = lax.axis_index("seq")
    levels = [segments]
    while segments.shape[0] > 2:
        earlier = segments[0::2]
        later = segments[1::2]
        joined = jnp.einsum(
            "phij,phjk->phik",
            later[:, :head_count],
            jnp.concatenate([earlier[:, :head_count], earlier[:, head_count:]], axis=-1),
            precision=precise_variant,
        )
        segments = jnp.concatenate(
            [joined[..., :DK], joined[..., DK:] + later[:, head_count:]], axis=1
        )
        levels.append(segments)
    opening_state = init_state
    cursor = 0
    for level in reversed(range(len(levels))):
        span = 2**level
        taken = (position // span) % 2 == 1
        piece = lax.dynamic_index_in_dim(levels[level], cursor // span, 0, keepdims=False)
        advanced = batch_product(piece[:head_count], opening_state) + piece[head_count:]
        opening_state = jnp.where(taken, advanced, opening_state)
        cursor = cursor + jnp.where(taken, span, 0)
    core = batch_product(query_effective, opening_state) + core_local
    core = core.transpose(1, 0, 2)
    gate_rows = out_gate.astype(jnp.float32).reshape(length, head_count, DV)
    gated = (
        core
        * lax.rsqrt(jnp.mean(core * core, axis=-1, keepdims=True) + 1e-06)
        * norm_gain
        * jax.nn.silu(gate_rows)
    )
    gated = gated.astype(jnp.bfloat16).reshape(length, head_count * DV)
    attn_part = jnp.dot(gated, out_proj, preferred_element_type=jnp.float32)
    share_width = model_width // lax.axis_size("head")
    share_start = lax.axis_index("head") * share_width
    column_total = lax.axis_size("head")
    attn_pieces = attn_part.astype(jnp.bfloat16).reshape(length, column_total, share_width)
    attn_pieces = lax.all_to_all(
        attn_pieces.transpose(1, 0, 2), "head", split_axis=0, concat_axis=0, tiled=True
    )
    attn_share = jnp.sum(attn_pieces.astype(jnp.float32), axis=0)
    stream_share = lax.dynamic_slice_in_dim(stream, share_start, share_width, 1)
    resid_share = (stream_share.astype(jnp.float32) + attn_share).astype(jnp.bfloat16)
    resid_share = lax.optimization_barrier(resid_share)
    resid_rows = lax.all_to_all(
        jnp.broadcast_to(resid_share[None], (column_total, length, share_width)),
        "head",
        split_axis=0,
        concat_axis=0,
        tiled=True,
    )
    resid = resid_rows.transpose(1, 0, 2).reshape(length, model_width)
    resid_f = resid.astype(jnp.float32)
    normed = (
        resid_f * lax.rsqrt(jnp.mean(resid_f * resid_f, axis=-1, keepdims=True) + 1e-06) * post_gain
    ).astype(jnp.bfloat16)
    peer_count = lax.axis_size("seq")
    column_count = lax.axis_size("head")
    expert_count = peer_count * column_count
    pick_count = expert_ids.shape[1]
    slot_count = min(length, length * pick_count * 2 // expert_count)
    targets = jnp.arange(peer_count, dtype=jnp.int32) * column_count + lax.axis_index("head")
    hits = expert_ids[:, :, None] == targets[None, None, :]
    weights = (route_scores / jnp.sum(route_scores, axis=1, keepdims=True)).astype(jnp.bfloat16)
    weights = lax.optimization_barrier(weights).astype(jnp.float32)
    chosen = jnp.sum(hits.astype(jnp.int32), axis=1)
    share_weight = jnp.sum(jnp.where(hits, weights[:, :, None], 0.0), axis=1)
    rank = jnp.cumsum(chosen, axis=0) - chosen
    slot_index = jnp.arange(slot_count, dtype=jnp.int32)
    placement_map = (
        (chosen[:, :, None] == 1) & (rank[:, :, None] == slot_index[None, None, :])
    ).astype(jnp.bfloat16)
    outgoing = jnp.einsum(
        "tps,td->psd", placement_map, normed, preferred_element_type=jnp.float32
    ).astype(jnp.bfloat16)
    incoming = lax.all_to_all(outgoing, "seq", split_axis=0, concat_axis=0, tiled=True)
    item_count = incoming.shape[1]
    flat_rows = incoming.reshape(-1, model_width)
    gate_e = jnp.dot(flat_rows, w_gate[0], preferred_element_type=jnp.float32)
    up_e = jnp.dot(flat_rows, w_up[0], preferred_element_type=jnp.float32)
    hidden = (jax.nn.silu(gate_e) * up_e).astype(jnp.bfloat16)
    result = jnp.dot(hidden, w_down[0], preferred_element_type=jnp.float32).astype(jnp.bfloat16)
    returned = lax.all_to_all(
        result.reshape(peer_count, item_count, model_width),
        "seq",
        split_axis=0,
        concat_axis=0,
        tiled=True,
    )
    combine_map = (placement_map.astype(jnp.float32) * share_weight[:, :, None]).astype(
        jnp.bfloat16
    )
    moe = jnp.einsum("tps,psd->td", combine_map, returned, preferred_element_type=jnp.float32)
    moe_pieces = moe.astype(jnp.bfloat16).reshape(length, column_total, share_width)
    moe_pieces = lax.all_to_all(
        moe_pieces.transpose(1, 0, 2), "head", split_axis=0, concat_axis=0, tiled=True
    )
    moe_share = jnp.sum(moe_pieces.astype(jnp.float32), axis=0)
    return (resid_share.astype(jnp.float32) + moe_share).astype(jnp.bfloat16)


def solution(mesh):
    return jax.shard_map(
        on_device,
        mesh=mesh,
        in_specs=(
            P(("dp", "seq"), None),
            P(("dp", "seq"), "head"),
            P(("dp", "seq"), "head"),
            P(("dp", "seq"), "head"),
            P(("dp", "seq"), "head"),
            P(("dp", "seq"), "head"),
            P(("dp", "seq"), "head"),
            P(("dp", "head"), None, None),
            P(),
            P("head", None),
            P(),
            P(("dp", "seq"), None),
            P(("dp", "seq"), None),
            P(("seq", "head"), None, None),
            P(("seq", "head"), None, None),
            P(("seq", "head"), None, None),
        ),
        out_specs=P(("dp", "seq"), "head"),
        check_vma=False,
    )
```

```python
import jax
import jax.numpy as jnp
from jax import lax
from jax.sharding import PartitionSpec as P

VALUE_HEAD_COUNT = 32
QK_HEADS = 16
DK = 128
DV = 128


precise_variant = lax.Precision.HIGHEST


def unit_rows(matrix):
    return matrix * lax.rsqrt(jnp.sum(matrix * matrix, axis=-1, keepdims=True) + 1e-06)


def batch_product(left, right):
    return jnp.einsum("hij,hjk->hik", left, right, precision=precise_variant)


def block_product(left, right):
    return jnp.einsum("...ij,...jk->...ik", left, right, precision=precise_variant)


def unit_lower_inverse(tri, block=16):
    heads, size_all, _ = tri.shape
    count = size_all // block
    eye_block = jnp.eye(block, dtype=tri.dtype)
    diagonal = jnp.stack(
        [tri[:, k * block : (k + 1) * block, k * block : (k + 1) * block] for k in range(count)],
        axis=1,
    )
    nil = diagonal - eye_block
    power = block_product(nil, nil)
    inverse = block_product(eye_block - nil, eye_block + power)
    reach = 4
    while reach < block:
        power = block_product(power, power)
        inverse = block_product(inverse, eye_block + power)
        reach *= 2
    size = block
    while size < size_all:
        pairs = inverse.shape[1] // 2
        first = inverse[:, 0::2]
        second = inverse[:, 1::2]
        coupling = jnp.stack(
            [
                tri[:, (2 * k + 1) * size : (2 * k + 2) * size, 2 * k * size : (2 * k + 1) * size]
                for k in range(pairs)
            ],
            axis=1,
        )
        lower_left = -block_product(second, block_product(coupling, first))
        top = jnp.concatenate([first, jnp.zeros_like(first)], axis=-1)
        bottom = jnp.concatenate([lower_left, second], axis=-1)
        inverse = jnp.concatenate([top, bottom], axis=-2)
        size *= 2
    return inverse[:, 0]


def on_device(
    stream,
    queries,
    keys,
    values,
    out_gate,
    gates,
    betas,
    init_state,
    norm_gain,
    out_proj,
    post_gain,
    expert_ids,
    route_scores,
    w_gate,
    w_up,
    w_down,
):
    length = stream.shape[0]
    model_width = stream.shape[1]
    head_count = values.shape[1] // DV
    group_size = VALUE_HEAD_COUNT // QK_HEADS
    scaled_q = unit_rows(queries.astype(jnp.float32).reshape(length, -1, DK)) * DK ** (-0.5)
    query_head_rows = jnp.repeat(scaled_q, group_size, axis=1).transpose(1, 0, 2)
    unit_k = unit_rows(keys.astype(jnp.float32).reshape(length, -1, DK))
    key_heads = jnp.repeat(unit_k, group_size, axis=1).transpose(1, 0, 2)
    value_heads = values.astype(jnp.float32).reshape(length, head_count, DV).transpose(1, 0, 2)
    beta_heads = betas.T
    log_decay = jnp.cumsum(jnp.log(gates), axis=0).T
    row_index = lax.broadcasted_iota(jnp.int32, (length, length), 0)
    col_index = lax.broadcasted_iota(jnp.int32, (length, length), 1)
    lower = row_index >= col_index
    strict = row_index > col_index
    gap_log = log_decay[:, :, None] - log_decay[:, None, :]
    decay = jnp.where(lower, jnp.exp(jnp.where(lower, gap_log, 0.0)), 0.0)
    key_inner = jnp.einsum("htk,hsk->hts", key_heads, key_heads, precision=precise_variant)
    tri_matrix = jnp.where(strict, decay * key_inner, 0.0) * beta_heads[:, :, None] + jnp.eye(
        length, dtype=jnp.float32
    )
    decay_factor = jnp.exp(log_decay)
    right_side = jnp.concatenate(
        [beta_heads[:, :, None] * value_heads, (beta_heads * decay_factor)[:, :, None] * key_heads],
        axis=-1,
    )
    solved = batch_product(unit_lower_inverse(tri_matrix), right_side)
    new_contribution = solved[:, :, :DV]
    carried_state = solved[:, :, DV:]
    tail_decay = jnp.exp(log_decay[:, -1:] - log_decay)
    keys_weighted = key_heads * tail_decay[:, :, None]
    eye_keys = jnp.eye(DK, dtype=jnp.float32)
    state_map = decay_factor[:, -1][:, None, None] * eye_keys - jnp.einsum(
        "htk,htj->hkj", keys_weighted, carried_state, precision=precise_variant
    )
    state_increment = jnp.einsum(
        "iys,iyn->isn", keys_weighted, new_contribution, precision=precise_variant
    )

    query_inner = (
        jnp.einsum("htk,hsk->hts", query_head_rows, key_heads, precision=precise_variant) * decay
    )
    query_effective = query_head_rows * decay_factor[:, :, None] - batch_product(
        query_inner, carried_state
    )
    core_local = batch_product(query_inner, new_contribution)
    own_pair = jnp.concatenate([state_map, state_increment], axis=0).astype(jnp.bfloat16)
    ring = lax.axis_size("seq")
    position = lax.axis_index("seq")
    forward_pairs = [(j, (j + 1) % ring) for j in range(ring)]
    backward_pairs = [(j, (j - 1) % ring) for j in range(ring)]
    pairs = jnp.zeros((ring,) + own_pair.shape, own_pair.dtype)
    pairs = lax.dynamic_update_index_in_dim(pairs, own_pair, position, 0)
    going_up = own_pair
    going_down = own_pair
    for step in range(1, ring // 2 + 1):
        going_up = lax.ppermute(going_up, "seq", forward_pairs)
        pairs = lax.dynamic_update_index_in_dim(pairs, going_up, (position - step) % ring, 0)
        if step < ring - step:
            going_down = lax.ppermute(going_down, "seq", backward_pairs)
            pairs = lax.dynamic_update_index_in_dim(
                pairs, going_down, (position + step) % ring, 0
            )
    segments = pairs.astype(jnp.float32)
    levels = [segments]
    while segments.shape[0] > 2:
        earlier = segments[0::2]
        later = segments[1::2]
        joined = jnp.einsum(
            "phij,phjk->phik",
            later[:, :head_count],
            jnp.concatenate([earlier[:, :head_count], earlier[:, head_count:]], axis=-1),
            precision=precise_variant,
        )
        segments = jnp.concatenate(
            [joined[..., :DK], joined[..., DK:] + later[:, head_count:]], axis=1
        )
        levels.append(segments)
    opening_state = init_state
    cursor = 0
    for level in reversed(range(len(levels))):
        span = 2**level
        taken = (position // span) % 2 == 1
        piece = lax.dynamic_index_in_dim(levels[level], cursor // span, 0, keepdims=False)
        advanced = batch_product(piece[:head_count], opening_state) + piece[head_count:]
        opening_state = jnp.where(taken, advanced, opening_state)
        cursor = cursor + jnp.where(taken, span, 0)
    core = batch_product(query_effective, opening_state) + core_local
    core = core.transpose(1, 0, 2)
    gate_rows = out_gate.astype(jnp.float32).reshape(length, head_count, DV)
    gated = (
        core
        * lax.rsqrt(jnp.mean(core * core, axis=-1, keepdims=True) + 1e-06)
        * norm_gain
        * jax.nn.silu(gate_rows)
    )
    gated = gated.astype(jnp.bfloat16).reshape(length, head_count * DV)
    attn_part = jnp.dot(gated, out_proj, preferred_element_type=jnp.float32)
    share_width = model_width // lax.axis_size("head")
    share_start = lax.axis_index("head") * share_width
    column_total = lax.axis_size("head")
    attn_pieces = attn_part.astype(jnp.bfloat16).reshape(length, column_total, share_width)
    attn_pieces = lax.all_to_all(
        attn_pieces.transpose(1, 0, 2), "head", split_axis=0, concat_axis=0, tiled=True
    )
    attn_share = jnp.sum(attn_pieces.astype(jnp.float32), axis=0)
    stream_share = lax.dynamic_slice_in_dim(stream, share_start, share_width, 1)
    resid_share = (stream_share.astype(jnp.float32) + attn_share).astype(jnp.bfloat16)
    resid_share = lax.optimization_barrier(resid_share)
    resid_rows = lax.all_to_all(
        jnp.broadcast_to(resid_share[None], (column_total, length, share_width)),
        "head",
        split_axis=0,
        concat_axis=0,
        tiled=True,
    )
    resid = resid_rows.transpose(1, 0, 2).reshape(length, model_width)
    resid_f = resid.astype(jnp.float32)
    normed = (
        resid_f * lax.rsqrt(jnp.mean(resid_f * resid_f, axis=-1, keepdims=True) + 1e-06) * post_gain
    ).astype(jnp.bfloat16)
    peer_count = lax.axis_size("seq")
    column_count = lax.axis_size("head")
    expert_count = peer_count * column_count
    pick_count = expert_ids.shape[1]
    slot_count = min(length, length * pick_count * 2 // expert_count)
    targets = jnp.arange(peer_count, dtype=jnp.int32) * column_count + lax.axis_index("head")
    hits = expert_ids[:, :, None] == targets[None, None, :]
    weights = (route_scores / jnp.sum(route_scores, axis=1, keepdims=True)).astype(jnp.bfloat16)
    weights = lax.optimization_barrier(weights).astype(jnp.float32)
    chosen = jnp.sum(hits.astype(jnp.int32), axis=1)
    share_weight = jnp.sum(jnp.where(hits, weights[:, :, None], 0.0), axis=1)
    rank = jnp.cumsum(chosen, axis=0) - chosen
    slot_index = jnp.arange(slot_count, dtype=jnp.int32)
    placement_map = (
        (chosen[:, :, None] == 1) & (rank[:, :, None] == slot_index[None, None, :])
    ).astype(jnp.bfloat16)
    outgoing = jnp.einsum(
        "tps,td->psd", placement_map, normed, preferred_element_type=jnp.float32
    ).astype(jnp.bfloat16)
    incoming = lax.all_to_all(outgoing, "seq", split_axis=0, concat_axis=0, tiled=True)
    item_count = incoming.shape[1]
    flat_rows = incoming.reshape(-1, model_width)
    gate_e = jnp.dot(flat_rows, w_gate[0], preferred_element_type=jnp.float32)
    up_e = jnp.dot(flat_rows, w_up[0], preferred_element_type=jnp.float32)
    hidden = (jax.nn.silu(gate_e) * up_e).astype(jnp.bfloat16)
    result = jnp.dot(hidden, w_down[0], preferred_element_type=jnp.float32).astype(jnp.bfloat16)
    returned = lax.all_to_all(
        result.reshape(peer_count, item_count, model_width),
        "seq",
        split_axis=0,
        concat_axis=0,
        tiled=True,
    )
    combine_map = (placement_map.astype(jnp.float32) * share_weight[:, :, None]).astype(
        jnp.bfloat16
    )
    moe = jnp.einsum("tps,psd->td", combine_map, returned, preferred_element_type=jnp.float32)
    moe_pieces = moe.astype(jnp.bfloat16).reshape(length, column_total, share_width)
    moe_pieces = lax.all_to_all(
        moe_pieces.transpose(1, 0, 2), "head", split_axis=0, concat_axis=0, tiled=True
    )
    moe_share = jnp.sum(moe_pieces.astype(jnp.float32), axis=0)
    return (resid_share.astype(jnp.float32) + moe_share).astype(jnp.bfloat16)


def solution(mesh):
    return jax.shard_map(
        on_device,
        mesh=mesh,
        in_specs=(
            P(("dp", "seq"), None),
            P(("dp", "seq"), "head"),
            P(("dp", "seq"), "head"),
            P(("dp", "seq"), "head"),
            P(("dp", "seq"), "head"),
            P(("dp", "seq"), "head"),
            P(("dp", "seq"), "head"),
            P(("dp", "head"), None, None),
            P(),
            P("head", None),
            P(),
            P(("dp", "seq"), None),
            P(("dp", "seq"), None),
            P(("seq", "head"), None, None),
            P(("seq", "head"), None, None),
            P(("seq", "head"), None, None),
        ),
        out_specs=P(("dp", "seq"), "head"),
        check_vma=False,
    )
```

```python
import jax
import jax.numpy as jnp
from jax import lax
from jax.sharding import PartitionSpec as P

VALUE_HEAD_COUNT = 32
QK_HEADS = 16
DK = 128
DV = 128


precise_variant = lax.Precision.HIGHEST


def unit_rows(matrix):
    return matrix * lax.rsqrt(jnp.sum(matrix * matrix, axis=-1, keepdims=True) + 1e-06)


def batch_product(left, right):
    return jnp.einsum("hij,hjk->hik", left, right, precision=precise_variant)


def batch_product_wide(left, right_a, right_b):
    joined = jnp.einsum(
        "hij,hjk->hik",
        left,
        jnp.concatenate([right_a, right_b], axis=-1),
        precision=precise_variant,
    )
    return joined


def block_product(left, right):
    return jnp.einsum("...ij,...jk->...ik", left, right, precision=precise_variant)


def unit_lower_inverse(tri, block=16):
    heads, size_all, _ = tri.shape
    count = size_all // block
    eye_block = jnp.eye(block, dtype=tri.dtype)
    diagonal = jnp.stack(
        [tri[:, k * block : (k + 1) * block, k * block : (k + 1) * block] for k in range(count)],
        axis=1,
    )
    nil = diagonal - eye_block
    power = block_product(nil, nil)
    inverse = block_product(eye_block - nil, eye_block + power)
    reach = 4
    while reach < block:
        power = block_product(power, power)
        inverse = block_product(inverse, eye_block + power)
        reach *= 2
    size = block
    while size < size_all:
        pairs = inverse.shape[1] // 2
        first = inverse[:, 0::2]
        second = inverse[:, 1::2]
        coupling = jnp.stack(
            [
                tri[:, (2 * k + 1) * size : (2 * k + 2) * size, 2 * k * size : (2 * k + 1) * size]
                for k in range(pairs)
            ],
            axis=1,
        )
        lower_left = -block_product(second, block_product(coupling, first))
        top = jnp.concatenate([first, jnp.zeros_like(first)], axis=-1)
        bottom = jnp.concatenate([lower_left, second], axis=-1)
        inverse = jnp.concatenate([top, bottom], axis=-2)
        size *= 2
    return inverse[:, 0]


def on_device(
    stream,
    queries,
    keys,
    values,
    out_gate,
    gates,
    betas,
    init_state,
    norm_gain,
    out_proj,
    post_gain,
    expert_ids,
    route_scores,
    w_gate,
    w_up,
    w_down,
):
    length = stream.shape[0]
    model_width = stream.shape[1]
    head_count = values.shape[1] // DV
    group_size = VALUE_HEAD_COUNT // QK_HEADS
    scaled_q = unit_rows(queries.astype(jnp.float32).reshape(length, -1, DK)) * DK ** (-0.5)
    query_head_rows = jnp.repeat(scaled_q, group_size, axis=1).transpose(1, 0, 2)
    unit_k = unit_rows(keys.astype(jnp.float32).reshape(length, -1, DK))
    key_heads = jnp.repeat(unit_k, group_size, axis=1).transpose(1, 0, 2)
    value_heads = values.astype(jnp.float32).reshape(length, head_count, DV).transpose(1, 0, 2)
    beta_heads = betas.T
    log_decay = jnp.cumsum(jnp.log(gates), axis=0).T
    row_index = lax.broadcasted_iota(jnp.int32, (length, length), 0)
    col_index = lax.broadcasted_iota(jnp.int32, (length, length), 1)
    lower = row_index >= col_index
    strict = row_index > col_index
    gap_log = log_decay[:, :, None] - log_decay[:, None, :]
    decay = jnp.where(lower, jnp.exp(jnp.where(lower, gap_log, 0.0)), 0.0)
    key_inner = jnp.einsum("htk,hsk->hts", key_heads, key_heads, precision=precise_variant)
    tri_matrix = jnp.where(strict, decay * key_inner, 0.0) * beta_heads[:, :, None] + jnp.eye(
        length, dtype=jnp.float32
    )
    decay_factor = jnp.exp(log_decay)
    right_side = jnp.concatenate(
        [beta_heads[:, :, None] * value_heads, (beta_heads * decay_factor)[:, :, None] * key_heads],
        axis=-1,
    )
    solved = batch_product(unit_lower_inverse(tri_matrix), right_side)
    new_contribution = solved[:, :, :DV]
    carried_state = solved[:, :, DV:]
    tail_decay = jnp.exp(log_decay[:, -1:] - log_decay)
    keys_weighted = key_heads * tail_decay[:, :, None]
    eye_keys = jnp.eye(DK, dtype=jnp.float32)
    state_map = decay_factor[:, -1][:, None, None] * eye_keys - jnp.einsum(
        "htk,htj->hkj", keys_weighted, carried_state, precision=precise_variant
    )
    state_increment = jnp.einsum(
        "iys,iyn->isn", keys_weighted, new_contribution, precision=precise_variant
    )

    query_inner = (
        jnp.einsum("htk,hsk->hts", query_head_rows, key_heads, precision=precise_variant) * decay
    )
    query_effective = query_head_rows * decay_factor[:, :, None] - batch_product(
        query_inner, carried_state
    )
    core_local = batch_product(query_inner, new_contribution)
    own_pair = jnp.concatenate([state_map, state_increment], axis=0).astype(jnp.bfloat16)
    ring = lax.axis_size("seq")
    position = lax.axis_index("seq")
    forward_pairs = [(j, (j + 1) % ring) for j in range(ring)]
    backward_pairs = [(j, (j - 1) % ring) for j in range(ring)]
    going_up = own_pair
    going_down = own_pair
    later_map = None
    later_add = None
    opening_state = init_state
    for step in range(1, ring // 2 + 1):
        going_up = lax.ppermute(going_up, "seq", forward_pairs)
        piece = going_up.astype(jnp.float32)
        if later_map is None:
            later_map = piece[:head_count]
            later_add = piece[head_count:]
        else:
            joined = batch_product_wide(later_map, piece[:head_count], piece[head_count:])
            useful = step <= position
            later_add = jnp.where(useful, joined[..., DK:] + later_add, later_add)
            later_map = jnp.where(useful, joined[..., :DK], later_map)
        if step < ring - step:
            going_down = lax.ppermute(going_down, "seq", backward_pairs)
            piece = going_down.astype(jnp.float32)
            advanced = batch_product(piece[:head_count], opening_state) + piece[head_count:]
            opening_state = jnp.where(position + step >= ring, advanced, opening_state)
    carried_open = batch_product(later_map, opening_state) + later_add
    opening_state = jnp.where(position > 0, carried_open, opening_state)
    core = batch_product(query_effective, opening_state) + core_local
    core = core.transpose(1, 0, 2)
    gate_rows = out_gate.astype(jnp.float32).reshape(length, head_count, DV)
    gated = (
        core
        * lax.rsqrt(jnp.mean(core * core, axis=-1, keepdims=True) + 1e-06)
        * norm_gain
        * jax.nn.silu(gate_rows)
    )
    gated = gated.astype(jnp.bfloat16).reshape(length, head_count * DV)
    attn_part = jnp.dot(gated, out_proj, preferred_element_type=jnp.float32)
    share_width = model_width // lax.axis_size("head")
    share_start = lax.axis_index("head") * share_width
    column_total = lax.axis_size("head")
    attn_pieces = attn_part.astype(jnp.bfloat16).reshape(length, column_total, share_width)
    attn_pieces = lax.all_to_all(
        attn_pieces.transpose(1, 0, 2), "head", split_axis=0, concat_axis=0, tiled=True
    )
    attn_share = jnp.sum(attn_pieces.astype(jnp.float32), axis=0)
    stream_share = lax.dynamic_slice_in_dim(stream, share_start, share_width, 1)
    resid_share = (stream_share.astype(jnp.float32) + attn_share).astype(jnp.bfloat16)
    resid_share = lax.optimization_barrier(resid_share)
    resid_rows = lax.all_to_all(
        jnp.broadcast_to(resid_share[None], (column_total, length, share_width)),
        "head",
        split_axis=0,
        concat_axis=0,
        tiled=True,
    )
    resid = resid_rows.transpose(1, 0, 2).reshape(length, model_width)
    resid_f = resid.astype(jnp.float32)
    normed = (
        resid_f * lax.rsqrt(jnp.mean(resid_f * resid_f, axis=-1, keepdims=True) + 1e-06) * post_gain
    ).astype(jnp.bfloat16)
    peer_count = lax.axis_size("seq")
    column_count = lax.axis_size("head")
    expert_count = peer_count * column_count
    pick_count = expert_ids.shape[1]
    slot_count = min(length, length * pick_count * 2 // expert_count)
    targets = jnp.arange(peer_count, dtype=jnp.int32) * column_count + lax.axis_index("head")
    hits = expert_ids[:, :, None] == targets[None, None, :]
    weights = (route_scores / jnp.sum(route_scores, axis=1, keepdims=True)).astype(jnp.bfloat16)
    weights = lax.optimization_barrier(weights).astype(jnp.float32)
    chosen = jnp.sum(hits.astype(jnp.int32), axis=1)
    share_weight = jnp.sum(jnp.where(hits, weights[:, :, None], 0.0), axis=1)
    rank = jnp.cumsum(chosen, axis=0) - chosen
    slot_index = jnp.arange(slot_count, dtype=jnp.int32)
    placement_map = (
        (chosen[:, :, None] == 1) & (rank[:, :, None] == slot_index[None, None, :])
    ).astype(jnp.bfloat16)
    outgoing = jnp.einsum(
        "tps,td->psd", placement_map, normed, preferred_element_type=jnp.float32
    ).astype(jnp.bfloat16)
    incoming = lax.all_to_all(outgoing, "seq", split_axis=0, concat_axis=0, tiled=True)
    gate_e = jnp.einsum("psd,dh->psh", incoming, w_gate[0], preferred_element_type=jnp.float32)
    up_e = jnp.einsum("psd,dh->psh", incoming, w_up[0], preferred_element_type=jnp.float32)
    hidden = (jax.nn.silu(gate_e) * up_e).astype(jnp.bfloat16)
    result = jnp.einsum(
        "psh,hd->psd", hidden, w_down[0], preferred_element_type=jnp.float32
    ).astype(jnp.bfloat16)
    returned = lax.all_to_all(
        result,
        "seq",
        split_axis=0,
        concat_axis=0,
        tiled=True,
    )
    combine_map = (placement_map.astype(jnp.float32) * share_weight[:, :, None]).astype(
        jnp.bfloat16
    )
    moe = jnp.einsum("tps,psd->td", combine_map, returned, preferred_element_type=jnp.float32)
    moe_pieces = moe.astype(jnp.bfloat16).reshape(length, column_total, share_width)
    moe_pieces = lax.all_to_all(
        moe_pieces.transpose(1, 0, 2), "head", split_axis=0, concat_axis=0, tiled=True
    )
    moe_share = jnp.sum(moe_pieces.astype(jnp.float32), axis=0)
    return (resid_share.astype(jnp.float32) + moe_share).astype(jnp.bfloat16)


def solution(mesh):
    return jax.shard_map(
        on_device,
        mesh=mesh,
        in_specs=(
            P(("dp", "seq"), None),
            P(("dp", "seq"), "head"),
            P(("dp", "seq"), "head"),
            P(("dp", "seq"), "head"),
            P(("dp", "seq"), "head"),
            P(("dp", "seq"), "head"),
            P(("dp", "seq"), "head"),
            P(("dp", "head"), None, None),
            P(),
            P("head", None),
            P(),
            P(("dp", "seq"), None),
            P(("dp", "seq"), None),
            P(("seq", "head"), None, None),
            P(("seq", "head"), None, None),
            P(("seq", "head"), None, None),
        ),
        out_specs=P(("dp", "seq"), "head"),
        check_vma=False,
    )
```

```python
import jax
import jax.numpy as jnp
from jax import lax
from jax.sharding import PartitionSpec as P

VALUE_HEAD_COUNT = 32
QK_HEADS = 16
DK = 128
DV = 128


precise_variant = lax.Precision.HIGHEST


def unit_rows(matrix):
    return matrix * lax.rsqrt(jnp.sum(matrix * matrix, axis=-1, keepdims=True) + 1e-06)


def batch_product(left, right):
    return jnp.einsum("hij,hjk->hik", left, right, precision=precise_variant)


def batch_product_wide(left, right_a, right_b):
    joined = jnp.einsum(
        "hij,hjk->hik",
        left,
        jnp.concatenate([right_a, right_b], axis=-1),
        precision=precise_variant,
    )
    return joined


def block_product(left, right):
    return jnp.einsum("...ij,...jk->...ik", left, right, precision=precise_variant)


def unit_lower_inverse(tri, block=16):
    heads, size_all, _ = tri.shape
    count = size_all // block
    eye_block = jnp.eye(block, dtype=tri.dtype)
    diagonal = jnp.stack(
        [tri[:, k * block : (k + 1) * block, k * block : (k + 1) * block] for k in range(count)],
        axis=1,
    )
    nil = diagonal - eye_block
    power = block_product(nil, nil)
    inverse = block_product(eye_block - nil, eye_block + power)
    reach = 4
    while reach < block:
        power = block_product(power, power)
        inverse = block_product(inverse, eye_block + power)
        reach *= 2
    size = block
    while size < size_all:
        pairs = inverse.shape[1] // 2
        first = inverse[:, 0::2]
        second = inverse[:, 1::2]
        coupling = jnp.stack(
            [
                tri[:, (2 * k + 1) * size : (2 * k + 2) * size, 2 * k * size : (2 * k + 1) * size]
                for k in range(pairs)
            ],
            axis=1,
        )
        lower_left = -block_product(second, block_product(coupling, first))
        top = jnp.concatenate([first, jnp.zeros_like(first)], axis=-1)
        bottom = jnp.concatenate([lower_left, second], axis=-1)
        inverse = jnp.concatenate([top, bottom], axis=-2)
        size *= 2
    return inverse[:, 0]


def on_device(
    stream,
    queries,
    keys,
    values,
    out_gate,
    gates,
    betas,
    init_state,
    norm_gain,
    out_proj,
    post_gain,
    expert_ids,
    route_scores,
    w_gate,
    w_up,
    w_down,
):
    length = stream.shape[0]
    model_width = stream.shape[1]
    head_count = values.shape[1] // DV
    group_size = VALUE_HEAD_COUNT // QK_HEADS
    scaled_q = unit_rows(queries.astype(jnp.float32).reshape(length, -1, DK)) * DK ** (-0.5)
    query_head_rows = jnp.repeat(scaled_q, group_size, axis=1).transpose(1, 0, 2)
    unit_k = unit_rows(keys.astype(jnp.float32).reshape(length, -1, DK))
    key_heads = jnp.repeat(unit_k, group_size, axis=1).transpose(1, 0, 2)
    value_heads = values.astype(jnp.float32).reshape(length, head_count, DV).transpose(1, 0, 2)
    beta_heads = betas.T
    log_decay = jnp.cumsum(jnp.log(gates), axis=0).T
    row_index = lax.broadcasted_iota(jnp.int32, (length, length), 0)
    col_index = lax.broadcasted_iota(jnp.int32, (length, length), 1)
    lower = row_index >= col_index
    strict = row_index > col_index
    gap_log = log_decay[:, :, None] - log_decay[:, None, :]
    decay = jnp.where(lower, jnp.exp(jnp.where(lower, gap_log, 0.0)), 0.0)
    key_inner = jnp.einsum("htk,hsk->hts", key_heads, key_heads, precision=precise_variant)
    tri_matrix = jnp.where(strict, decay * key_inner, 0.0) * beta_heads[:, :, None] + jnp.eye(
        length, dtype=jnp.float32
    )
    decay_factor = jnp.exp(log_decay)
    right_side = jnp.concatenate(
        [beta_heads[:, :, None] * value_heads, (beta_heads * decay_factor)[:, :, None] * key_heads],
        axis=-1,
    )
    solved = batch_product(unit_lower_inverse(tri_matrix), right_side)
    new_contribution = solved[:, :, :DV]
    carried_state = solved[:, :, DV:]
    tail_decay = jnp.exp(log_decay[:, -1:] - log_decay)
    keys_weighted = key_heads * tail_decay[:, :, None]
    eye_keys = jnp.eye(DK, dtype=jnp.float32)
    state_map = decay_factor[:, -1][:, None, None] * eye_keys - jnp.einsum(
        "htk,htj->hkj", keys_weighted, carried_state, precision=precise_variant
    )
    state_increment = jnp.einsum(
        "iys,iyn->isn", keys_weighted, new_contribution, precision=precise_variant
    )

    query_inner = (
        jnp.einsum("htk,hsk->hts", query_head_rows, key_heads, precision=precise_variant) * decay
    )
    query_effective = query_head_rows * decay_factor[:, :, None] - batch_product(
        query_inner, carried_state
    )
    core_local = batch_product(query_inner, new_contribution)
    own_pair = jnp.concatenate([state_map, state_increment], axis=0).astype(jnp.bfloat16)
    ring = lax.axis_size("seq")
    position = lax.axis_index("seq")
    forward_pairs = [(j, (j + 1) % ring) for j in range(ring)]
    backward_pairs = [(j, (j - 1) % ring) for j in range(ring)]
    going_up = own_pair
    going_down = own_pair
    later_map = None
    later_add = None
    opening_state = init_state
    for step in range(1, ring // 2 + 1):
        going_up = lax.ppermute(going_up, "seq", forward_pairs)
        piece = going_up.astype(jnp.float32)
        if later_map is None:
            later_map = piece[:head_count]
            later_add = piece[head_count:]
        else:
            joined = batch_product_wide(later_map, piece[:head_count], piece[head_count:])
            useful = step <= position
            later_add = jnp.where(useful, joined[..., DK:] + later_add, later_add)
            later_map = jnp.where(useful, joined[..., :DK], later_map)
        if step < ring - step:
            going_down = lax.ppermute(going_down, "seq", backward_pairs)
            piece = going_down.astype(jnp.float32)
            advanced = batch_product(piece[:head_count], opening_state) + piece[head_count:]
            opening_state = jnp.where(position + step >= ring, advanced, opening_state)
    carried_open = batch_product(later_map, opening_state) + later_add
    opening_state = jnp.where(position > 0, carried_open, opening_state)
    core = batch_product(query_effective, opening_state) + core_local
    core = core.transpose(1, 0, 2)
    gate_rows = out_gate.astype(jnp.float32).reshape(length, head_count, DV)
    gated = (
        core
        * lax.rsqrt(jnp.mean(core * core, axis=-1, keepdims=True) + 1e-06)
        * norm_gain
        * jax.nn.silu(gate_rows)
    )
    gated = gated.astype(jnp.bfloat16).reshape(length, head_count * DV)
    attn_part = jnp.dot(gated, out_proj, preferred_element_type=jnp.float32)
    share_width = model_width // lax.axis_size("head")
    share_start = lax.axis_index("head") * share_width
    column_total = lax.axis_size("head")
    attn_pieces = attn_part.astype(jnp.bfloat16).reshape(length, column_total, share_width)
    attn_pieces = lax.all_to_all(
        attn_pieces.transpose(1, 0, 2), "head", split_axis=0, concat_axis=0, tiled=True
    )
    attn_share = jnp.sum(attn_pieces.astype(jnp.float32), axis=0)
    stream_share = lax.dynamic_slice_in_dim(stream, share_start, share_width, 1)
    resid_share = (stream_share.astype(jnp.float32) + attn_share).astype(jnp.bfloat16)
    resid_share = lax.optimization_barrier(resid_share)
    resid_rows = lax.all_to_all(
        jnp.broadcast_to(resid_share[None], (column_total, length, share_width)),
        "head",
        split_axis=0,
        concat_axis=0,
        tiled=True,
    )
    resid = resid_rows.transpose(1, 0, 2).reshape(length, model_width)
    resid_f = resid.astype(jnp.float32)
    normed = (
        resid_f * lax.rsqrt(jnp.mean(resid_f * resid_f, axis=-1, keepdims=True) + 1e-06) * post_gain
    ).astype(jnp.bfloat16)
    peer_count = lax.axis_size("seq")
    column_count = lax.axis_size("head")
    expert_count = peer_count * column_count
    pick_count = expert_ids.shape[1]
    slot_count = min(length, length * pick_count * 2 // expert_count)
    offsets = jnp.arange(peer_count, dtype=jnp.int32)
    targets = ((lax.axis_index("seq") + offsets) % peer_count) * column_count + lax.axis_index(
        "head"
    )
    hits = expert_ids[:, :, None] == targets[None, None, :]
    weights = (route_scores / jnp.sum(route_scores, axis=1, keepdims=True)).astype(jnp.bfloat16)
    weights = lax.optimization_barrier(weights).astype(jnp.float32)
    chosen = jnp.sum(hits.astype(jnp.int32), axis=1)
    share_weight = jnp.sum(jnp.where(hits, weights[:, :, None], 0.0), axis=1)
    rank = jnp.cumsum(chosen, axis=0) - chosen
    slot_index = jnp.arange(slot_count, dtype=jnp.int32)
    placement_map = (
        (chosen[:, :, None] == 1) & (rank[:, :, None] == slot_index[None, None, :])
    ).astype(jnp.bfloat16)
    outgoing = jnp.einsum(
        "tps,td->psd", placement_map, normed, preferred_element_type=jnp.float32
    ).astype(jnp.bfloat16)
    incoming = jnp.stack(
        [outgoing[0]]
        + [
            lax.ppermute(
                outgoing[shift],
                "seq",
                [(j, (j + shift) % peer_count) for j in range(peer_count)],
            )
            for shift in range(1, peer_count)
        ]
    )
    gate_e = jnp.einsum("psd,dh->psh", incoming, w_gate[0], preferred_element_type=jnp.float32)
    up_e = jnp.einsum("psd,dh->psh", incoming, w_up[0], preferred_element_type=jnp.float32)
    hidden = (jax.nn.silu(gate_e) * up_e).astype(jnp.bfloat16)
    result = jnp.einsum(
        "psh,hd->psd", hidden, w_down[0], preferred_element_type=jnp.float32
    ).astype(jnp.bfloat16)
    returned = jnp.stack(
        [result[0]]
        + [
            lax.ppermute(
                result[shift],
                "seq",
                [((j + shift) % peer_count, j) for j in range(peer_count)],
            )
            for shift in range(1, peer_count)
        ]
    )
    combine_map = (placement_map.astype(jnp.float32) * share_weight[:, :, None]).astype(
        jnp.bfloat16
    )
    moe = jnp.einsum("tps,psd->td", combine_map, returned, preferred_element_type=jnp.float32)
    moe_pieces = moe.astype(jnp.bfloat16).reshape(length, column_total, share_width)
    moe_pieces = lax.all_to_all(
        moe_pieces.transpose(1, 0, 2), "head", split_axis=0, concat_axis=0, tiled=True
    )
    moe_share = jnp.sum(moe_pieces.astype(jnp.float32), axis=0)
    return (resid_share.astype(jnp.float32) + moe_share).astype(jnp.bfloat16)


def solution(mesh):
    return jax.shard_map(
        on_device,
        mesh=mesh,
        in_specs=(
            P(("dp", "seq"), None),
            P(("dp", "seq"), "head"),
            P(("dp", "seq"), "head"),
            P(("dp", "seq"), "head"),
            P(("dp", "seq"), "head"),
            P(("dp", "seq"), "head"),
            P(("dp", "seq"), "head"),
            P(("dp", "head"), None, None),
            P(),
            P("head", None),
            P(),
            P(("dp", "seq"), None),
            P(("dp", "seq"), None),
            P(("seq", "head"), None, None),
            P(("seq", "head"), None, None),
            P(("seq", "head"), None, None),
        ),
        out_specs=P(("dp", "seq"), "head"),
        check_vma=False,
    )
```

```python
import jax
import jax.numpy as jnp
from jax import lax
from jax.sharding import PartitionSpec as P

VALUE_HEAD_COUNT = 32
QK_HEADS = 16
DK = 128
DV = 128


precise_variant = lax.Precision.HIGHEST


def unit_rows(matrix):
    return matrix * lax.rsqrt(jnp.sum(matrix * matrix, axis=-1, keepdims=True) + 1e-06)


def batch_product(left, right):
    return jnp.einsum("hij,hjk->hik", left, right, precision=precise_variant)


def batch_product_wide(left, right_a, right_b):
    joined = jnp.einsum(
        "hij,hjk->hik",
        left,
        jnp.concatenate([right_a, right_b], axis=-1),
        precision=precise_variant,
    )
    return joined


def block_product(left, right):
    return jnp.einsum("...ij,...jk->...ik", left, right, precision=precise_variant)


def unit_lower_inverse(tri, block=16):
    heads, size_all, _ = tri.shape
    count = size_all // block
    eye_block = jnp.eye(block, dtype=tri.dtype)
    diagonal = jnp.stack(
        [tri[:, k * block : (k + 1) * block, k * block : (k + 1) * block] for k in range(count)],
        axis=1,
    )
    nil = diagonal - eye_block
    power = block_product(nil, nil)
    inverse = block_product(eye_block - nil, eye_block + power)
    reach = 4
    while reach < block:
        power = block_product(power, power)
        inverse = block_product(inverse, eye_block + power)
        reach *= 2
    size = block
    while size < size_all:
        pairs = inverse.shape[1] // 2
        first = inverse[:, 0::2]
        second = inverse[:, 1::2]
        coupling = jnp.stack(
            [
                tri[:, (2 * k + 1) * size : (2 * k + 2) * size, 2 * k * size : (2 * k + 1) * size]
                for k in range(pairs)
            ],
            axis=1,
        )
        lower_left = -block_product(second, block_product(coupling, first))
        top = jnp.concatenate([first, jnp.zeros_like(first)], axis=-1)
        bottom = jnp.concatenate([lower_left, second], axis=-1)
        inverse = jnp.concatenate([top, bottom], axis=-2)
        size *= 2
    return inverse[:, 0]


def on_device(
    stream,
    queries,
    keys,
    values,
    out_gate,
    gates,
    betas,
    init_state,
    norm_gain,
    out_proj,
    post_gain,
    expert_ids,
    route_scores,
    w_gate,
    w_up,
    w_down,
):
    length = stream.shape[0]
    model_width = stream.shape[1]
    head_count = values.shape[1] // DV
    group_size = VALUE_HEAD_COUNT // QK_HEADS
    scaled_q = unit_rows(queries.astype(jnp.float32).reshape(length, -1, DK)) * DK ** (-0.5)
    query_head_rows = jnp.repeat(scaled_q, group_size, axis=1).transpose(1, 0, 2)
    unit_k = unit_rows(keys.astype(jnp.float32).reshape(length, -1, DK))
    key_heads = jnp.repeat(unit_k, group_size, axis=1).transpose(1, 0, 2)
    value_heads = values.astype(jnp.float32).reshape(length, head_count, DV).transpose(1, 0, 2)
    beta_heads = betas.T
    log_decay = jnp.cumsum(jnp.log(gates), axis=0).T
    row_index = lax.broadcasted_iota(jnp.int32, (length, length), 0)
    col_index = lax.broadcasted_iota(jnp.int32, (length, length), 1)
    lower = row_index >= col_index
    strict = row_index > col_index
    gap_log = log_decay[:, :, None] - log_decay[:, None, :]
    decay = jnp.where(lower, jnp.exp(jnp.where(lower, gap_log, 0.0)), 0.0)
    key_inner = jnp.einsum("htk,hsk->hts", key_heads, key_heads, precision=precise_variant)
    tri_matrix = jnp.where(strict, decay * key_inner, 0.0) * beta_heads[:, :, None] + jnp.eye(
        length, dtype=jnp.float32
    )
    decay_factor = jnp.exp(log_decay)
    right_side = jnp.concatenate(
        [beta_heads[:, :, None] * value_heads, (beta_heads * decay_factor)[:, :, None] * key_heads],
        axis=-1,
    )
    solved = batch_product(unit_lower_inverse(tri_matrix), right_side)
    new_contribution = solved[:, :, :DV]
    carried_state = solved[:, :, DV:]
    tail_decay = jnp.exp(log_decay[:, -1:] - log_decay)
    keys_weighted = key_heads * tail_decay[:, :, None]
    eye_keys = jnp.eye(DK, dtype=jnp.float32)
    state_map = decay_factor[:, -1][:, None, None] * eye_keys - jnp.einsum(
        "htk,htj->hkj", keys_weighted, carried_state, precision=precise_variant
    )
    state_increment = jnp.einsum(
        "iys,iyn->isn", keys_weighted, new_contribution, precision=precise_variant
    )

    query_inner = (
        jnp.einsum("htk,hsk->hts", query_head_rows, key_heads, precision=precise_variant) * decay
    )
    query_effective = query_head_rows * decay_factor[:, :, None] - batch_product(
        query_inner, carried_state
    )
    core_local = batch_product(query_inner, new_contribution)
    own_pair = jnp.concatenate([state_map, state_increment], axis=0).astype(jnp.bfloat16)
    ring = lax.axis_size("seq")
    position = lax.axis_index("seq")
    forward_pairs = [(j, (j + 1) % ring) for j in range(ring)]
    backward_pairs = [(j, (j - 1) % ring) for j in range(ring)]
    going_up = own_pair
    going_down = own_pair
    later_map = None
    later_add = None
    opening_state = init_state
    for step in range(1, ring // 2 + 1):
        going_up = lax.ppermute(going_up, "seq", forward_pairs)
        piece = going_up.astype(jnp.float32)
        if later_map is None:
            later_map = piece[:head_count]
            later_add = piece[head_count:]
        else:
            joined = batch_product_wide(later_map, piece[:head_count], piece[head_count:])
            useful = step <= position
            later_add = jnp.where(useful, joined[..., DK:] + later_add, later_add)
            later_map = jnp.where(useful, joined[..., :DK], later_map)
        if step < ring - step:
            going_down = lax.ppermute(going_down, "seq", backward_pairs)
            piece = going_down.astype(jnp.float32)
            advanced = batch_product(piece[:head_count], opening_state) + piece[head_count:]
            opening_state = jnp.where(position + step >= ring, advanced, opening_state)
    carried_open = batch_product(later_map, opening_state) + later_add
    opening_state = jnp.where(position > 0, carried_open, opening_state)
    core = batch_product(query_effective, opening_state) + core_local
    core = core.transpose(1, 0, 2)
    gate_rows = out_gate.astype(jnp.float32).reshape(length, head_count, DV)
    gated = (
        core
        * lax.rsqrt(jnp.mean(core * core, axis=-1, keepdims=True) + 1e-06)
        * norm_gain
        * jax.nn.silu(gate_rows)
    )
    gated = gated.astype(jnp.bfloat16).reshape(length, head_count * DV)
    attn_part = jnp.dot(gated, out_proj, preferred_element_type=jnp.float32)
    share_width = model_width // lax.axis_size("head")
    share_start = lax.axis_index("head") * share_width
    column_total = lax.axis_size("head")
    attn_pieces = attn_part.astype(jnp.bfloat16).reshape(length, column_total, share_width)
    attn_pieces = lax.all_to_all(
        attn_pieces.transpose(1, 0, 2), "head", split_axis=0, concat_axis=0, tiled=True
    )
    attn_share = jnp.sum(attn_pieces.astype(jnp.float32), axis=0)
    stream_share = lax.dynamic_slice_in_dim(stream, share_start, share_width, 1)
    resid_share = (stream_share.astype(jnp.float32) + attn_share).astype(jnp.bfloat16)
    resid_share = lax.optimization_barrier(resid_share)
    resid_rows = lax.all_to_all(
        jnp.broadcast_to(resid_share[None], (column_total, length, share_width)),
        "head",
        split_axis=0,
        concat_axis=0,
        tiled=True,
    )
    resid = resid_rows.transpose(1, 0, 2).reshape(length, model_width)
    resid_f = resid.astype(jnp.float32)
    normed = (
        resid_f * lax.rsqrt(jnp.mean(resid_f * resid_f, axis=-1, keepdims=True) + 1e-06) * post_gain
    ).astype(jnp.bfloat16)
    peer_count = lax.axis_size("seq")
    column_count = lax.axis_size("head")
    expert_count = peer_count * column_count
    pick_count = expert_ids.shape[1]
    slot_count = min(length, length * pick_count * 2 // expert_count)
    targets = jnp.arange(peer_count, dtype=jnp.int32) * column_count + lax.axis_index("head")
    hits = expert_ids[:, :, None] == targets[None, None, :]
    weights = (route_scores / jnp.sum(route_scores, axis=1, keepdims=True)).astype(jnp.bfloat16)
    weights = lax.optimization_barrier(weights).astype(jnp.float32)
    chosen = jnp.sum(hits.astype(jnp.int32), axis=1)
    share_weight = jnp.sum(jnp.where(hits, weights[:, :, None], 0.0), axis=1)
    rank = jnp.cumsum(chosen, axis=0) - chosen
    slot_index = jnp.arange(slot_count, dtype=jnp.int32)
    placement_map = (
        (chosen[:, :, None] == 1) & (rank[:, :, None] == slot_index[None, None, :])
    ).astype(jnp.bfloat16)
    outgoing = jnp.einsum(
        "tps,td->psd", placement_map, normed, preferred_element_type=jnp.float32
    ).astype(jnp.bfloat16)
    incoming = lax.all_to_all(outgoing, "seq", split_axis=0, concat_axis=0, tiled=True)
    gate_e = jnp.einsum("psd,dh->psh", incoming, w_gate[0], preferred_element_type=jnp.float32)
    up_e = jnp.einsum("psd,dh->psh", incoming, w_up[0], preferred_element_type=jnp.float32)
    hidden = (jax.nn.silu(gate_e) * up_e).astype(jnp.bfloat16)
    result = jnp.einsum(
        "psh,hd->psd", hidden, w_down[0], preferred_element_type=jnp.float32
    ).astype(jnp.bfloat16)
    sliced = result.reshape(peer_count, slot_count, column_count, share_width)
    sliced = sliced.transpose(0, 2, 1, 3).reshape(expert_count, slot_count, share_width)
    returned = lax.all_to_all(sliced, ("seq", "head"), split_axis=0, concat_axis=0, tiled=True)
    every_expert = jnp.arange(expert_count, dtype=jnp.int32)
    hits_all = expert_ids[:, :, None] == every_expert[None, None, :]
    chosen_all = jnp.sum(hits_all.astype(jnp.int32), axis=1)
    weight_all = jnp.sum(jnp.where(hits_all, weights[:, :, None], 0.0), axis=1)
    rank_all = jnp.cumsum(chosen_all, axis=0) - chosen_all
    combine_all = jnp.where(
        (chosen_all[:, :, None] == 1) & (rank_all[:, :, None] == slot_index[None, None, :]),
        weight_all[:, :, None],
        0.0,
    ).astype(jnp.bfloat16)
    moe_share = jnp.einsum(
        "tes,esc->tc", combine_all, returned, preferred_element_type=jnp.float32
    )
    return (resid_share.astype(jnp.float32) + moe_share).astype(jnp.bfloat16)


def solution(mesh):
    return jax.shard_map(
        on_device,
        mesh=mesh,
        in_specs=(
            P(("dp", "seq"), None),
            P(("dp", "seq"), "head"),
            P(("dp", "seq"), "head"),
            P(("dp", "seq"), "head"),
            P(("dp", "seq"), "head"),
            P(("dp", "seq"), "head"),
            P(("dp", "seq"), "head"),
            P(("dp", "head"), None, None),
            P(),
            P("head", None),
            P(),
            P(("dp", "seq"), None),
            P(("dp", "seq"), None),
            P(("seq", "head"), None, None),
            P(("seq", "head"), None, None),
            P(("seq", "head"), None, None),
        ),
        out_specs=P(("dp", "seq"), "head"),
        check_vma=False,
    )
```

```python
import jax
import jax.numpy as jnp
from jax import lax
from jax.sharding import PartitionSpec as P

VALUE_HEAD_COUNT = 32
QK_HEADS = 16
DK = 128
DV = 128


precise_variant = lax.Precision.HIGHEST


def unit_rows(matrix):
    return matrix * lax.rsqrt(jnp.sum(matrix * matrix, axis=-1, keepdims=True) + 1e-06)


def batch_product(left, right):
    return jnp.einsum("hij,hjk->hik", left, right, precision=precise_variant)


def batch_product_wide(left, right_a, right_b):
    joined = jnp.einsum(
        "hij,hjk->hik",
        left,
        jnp.concatenate([right_a, right_b], axis=-1),
        precision=precise_variant,
    )
    return joined


def block_product(left, right):
    return jnp.einsum("...ij,...jk->...ik", left, right, precision=precise_variant)


def unit_lower_inverse(tri, block=16):
    heads, size_all, _ = tri.shape
    count = size_all // block
    eye_block = jnp.eye(block, dtype=tri.dtype)
    diagonal = jnp.stack(
        [tri[:, k * block : (k + 1) * block, k * block : (k + 1) * block] for k in range(count)],
        axis=1,
    )
    nil = diagonal - eye_block
    power = block_product(nil, nil)
    inverse = block_product(eye_block - nil, eye_block + power)
    reach = 4
    while reach < block:
        power = block_product(power, power)
        inverse = block_product(inverse, eye_block + power)
        reach *= 2
    size = block
    while size < size_all:
        pairs = inverse.shape[1] // 2
        first = inverse[:, 0::2]
        second = inverse[:, 1::2]
        coupling = jnp.stack(
            [
                tri[:, (2 * k + 1) * size : (2 * k + 2) * size, 2 * k * size : (2 * k + 1) * size]
                for k in range(pairs)
            ],
            axis=1,
        )
        lower_left = -block_product(second, block_product(coupling, first))
        top = jnp.concatenate([first, jnp.zeros_like(first)], axis=-1)
        bottom = jnp.concatenate([lower_left, second], axis=-1)
        inverse = jnp.concatenate([top, bottom], axis=-2)
        size *= 2
    return inverse[:, 0]


def on_device(
    stream,
    queries,
    keys,
    values,
    out_gate,
    gates,
    betas,
    init_state,
    norm_gain,
    out_proj,
    post_gain,
    expert_ids,
    route_scores,
    w_gate,
    w_up,
    w_down,
):
    length = stream.shape[0]
    model_width = stream.shape[1]
    head_count = values.shape[1] // DV
    group_size = VALUE_HEAD_COUNT // QK_HEADS
    scaled_q = unit_rows(queries.astype(jnp.float32).reshape(length, -1, DK)) * DK ** (-0.5)
    query_head_rows = jnp.repeat(scaled_q, group_size, axis=1).transpose(1, 0, 2)
    unit_k = unit_rows(keys.astype(jnp.float32).reshape(length, -1, DK))
    key_heads = jnp.repeat(unit_k, group_size, axis=1).transpose(1, 0, 2)
    value_heads = values.astype(jnp.float32).reshape(length, head_count, DV).transpose(1, 0, 2)
    beta_heads = betas.T
    log_decay = jnp.cumsum(jnp.log(gates), axis=0).T
    row_index = lax.broadcasted_iota(jnp.int32, (length, length), 0)
    col_index = lax.broadcasted_iota(jnp.int32, (length, length), 1)
    lower = row_index >= col_index
    strict = row_index > col_index
    gap_log = log_decay[:, :, None] - log_decay[:, None, :]
    decay = jnp.where(lower, jnp.exp(jnp.where(lower, gap_log, 0.0)), 0.0)
    key_inner = jnp.einsum("htk,hsk->hts", key_heads, key_heads, precision=precise_variant)
    tri_matrix = jnp.where(strict, decay * key_inner, 0.0) * beta_heads[:, :, None] + jnp.eye(
        length, dtype=jnp.float32
    )
    decay_factor = jnp.exp(log_decay)
    right_side = jnp.concatenate(
        [beta_heads[:, :, None] * value_heads, (beta_heads * decay_factor)[:, :, None] * key_heads],
        axis=-1,
    )
    solved = batch_product(unit_lower_inverse(tri_matrix), right_side)
    new_contribution = solved[:, :, :DV]
    carried_state = solved[:, :, DV:]
    tail_decay = jnp.exp(log_decay[:, -1:] - log_decay)
    keys_weighted = key_heads * tail_decay[:, :, None]
    eye_keys = jnp.eye(DK, dtype=jnp.float32)
    state_map = decay_factor[:, -1][:, None, None] * eye_keys - jnp.einsum(
        "htk,htj->hkj", keys_weighted, carried_state, precision=precise_variant
    )
    state_increment = jnp.einsum(
        "iys,iyn->isn", keys_weighted, new_contribution, precision=precise_variant
    )

    query_inner = (
        jnp.einsum("htk,hsk->hts", query_head_rows, key_heads, precision=precise_variant) * decay
    )
    query_effective = query_head_rows * decay_factor[:, :, None] - batch_product(
        query_inner, carried_state
    )
    core_local = batch_product(query_inner, new_contribution)
    own_pair = jnp.concatenate([state_map, state_increment], axis=0).astype(jnp.bfloat16)
    ring = lax.axis_size("seq")
    position = lax.axis_index("seq")
    forward_pairs = [(j, (j + 1) % ring) for j in range(ring)]
    backward_pairs = [(j, (j - 1) % ring) for j in range(ring)]
    going_up = own_pair
    going_down = own_pair
    later_map = None
    later_add = None
    opening_state = init_state
    for step in range(1, ring // 2 + 1):
        going_up = lax.ppermute(going_up, "seq", forward_pairs)
        piece = going_up.astype(jnp.float32)
        if later_map is None:
            later_map = piece[:head_count]
            later_add = piece[head_count:]
        else:
            joined = batch_product_wide(later_map, piece[:head_count], piece[head_count:])
            useful = step <= position
            later_add = jnp.where(useful, joined[..., DK:] + later_add, later_add)
            later_map = jnp.where(useful, joined[..., :DK], later_map)
        if step < ring - step:
            going_down = lax.ppermute(going_down, "seq", backward_pairs)
            piece = going_down.astype(jnp.float32)
            advanced = batch_product(piece[:head_count], opening_state) + piece[head_count:]
            opening_state = jnp.where(position + step >= ring, advanced, opening_state)
    carried_open = batch_product(later_map, opening_state) + later_add
    opening_state = jnp.where(position > 0, carried_open, opening_state)
    core = batch_product(query_effective, opening_state) + core_local
    core = core.transpose(1, 0, 2)
    gate_rows = out_gate.astype(jnp.float32).reshape(length, head_count, DV)
    gated = (
        core
        * lax.rsqrt(jnp.mean(core * core, axis=-1, keepdims=True) + 1e-06)
        * norm_gain
        * jax.nn.silu(gate_rows)
    )
    gated = gated.astype(jnp.bfloat16).reshape(length, head_count * DV)
    attn_part = jnp.dot(gated, out_proj, preferred_element_type=jnp.float32)
    share_width = model_width // lax.axis_size("head")
    share_start = lax.axis_index("head") * share_width
    column_total = lax.axis_size("head")
    attn_pieces = attn_part.astype(jnp.bfloat16).reshape(length, column_total, share_width)
    attn_pieces = lax.all_to_all(
        attn_pieces.transpose(1, 0, 2), "head", split_axis=0, concat_axis=0, tiled=True
    )
    attn_share = jnp.sum(attn_pieces.astype(jnp.float32), axis=0)
    stream_share = lax.dynamic_slice_in_dim(stream, share_start, share_width, 1)
    resid_share = (stream_share.astype(jnp.float32) + attn_share).astype(jnp.bfloat16)
    resid_share = lax.optimization_barrier(resid_share)
    resid_f = resid_share.astype(jnp.float32)
    square_part = jnp.sum(resid_f * resid_f, axis=-1)
    square_parts = lax.all_to_all(
        jnp.broadcast_to(square_part[None], (column_total, length)),
        "head",
        split_axis=0,
        concat_axis=0,
        tiled=True,
    )
    square_mean = jnp.sum(square_parts, axis=0) / model_width
    gain_share = lax.dynamic_slice_in_dim(post_gain, share_start, share_width, 0)
    normed_share = (
        resid_f * lax.rsqrt(square_mean[:, None] + 1e-06) * gain_share
    ).astype(jnp.bfloat16)
    peer_count = lax.axis_size("seq")
    column_count = lax.axis_size("head")
    expert_count = peer_count * column_count
    pick_count = expert_ids.shape[1]
    slot_count = min(length, length * pick_count * 2 // expert_count)
    weights = (route_scores / jnp.sum(route_scores, axis=1, keepdims=True)).astype(jnp.bfloat16)
    weights = lax.optimization_barrier(weights).astype(jnp.float32)
    slot_index = jnp.arange(slot_count, dtype=jnp.int32)
    every_expert = jnp.arange(expert_count, dtype=jnp.int32)
    hits_all = expert_ids[:, :, None] == every_expert[None, None, :]
    chosen_all = jnp.sum(hits_all.astype(jnp.int32), axis=1)
    weight_all = jnp.sum(jnp.where(hits_all, weights[:, :, None], 0.0), axis=1)
    rank_all = jnp.cumsum(chosen_all, axis=0) - chosen_all
    placed_all = (chosen_all[:, :, None] == 1) & (rank_all[:, :, None] == slot_index[None, None, :])
    outgoing = jnp.einsum(
        "tes,tc->esc",
        placed_all.astype(jnp.bfloat16),
        normed_share,
        preferred_element_type=jnp.float32,
    ).astype(jnp.bfloat16)
    gathered = lax.all_to_all(outgoing, ("seq", "head"), split_axis=0, concat_axis=0, tiled=True)
    incoming = (
        gathered.reshape(peer_count, column_count, slot_count, share_width)
        .transpose(0, 2, 1, 3)
        .reshape(peer_count, slot_count, model_width)
    )
    gate_e = jnp.einsum("psd,dh->psh", incoming, w_gate[0], preferred_element_type=jnp.float32)
    up_e = jnp.einsum("psd,dh->psh", incoming, w_up[0], preferred_element_type=jnp.float32)
    hidden = (jax.nn.silu(gate_e) * up_e).astype(jnp.bfloat16)
    result = jnp.einsum(
        "psh,hd->psd", hidden, w_down[0], preferred_element_type=jnp.float32
    ).astype(jnp.bfloat16)
    sliced = result.reshape(peer_count, slot_count, column_count, share_width)
    sliced = sliced.transpose(0, 2, 1, 3).reshape(expert_count, slot_count, share_width)
    returned = lax.all_to_all(sliced, ("seq", "head"), split_axis=0, concat_axis=0, tiled=True)
    combine_all = jnp.where(placed_all, weight_all[:, :, None], 0.0).astype(jnp.bfloat16)
    moe_share = jnp.einsum(
        "tes,esc->tc", combine_all, returned, preferred_element_type=jnp.float32
    )
    return (resid_share.astype(jnp.float32) + moe_share).astype(jnp.bfloat16)


def solution(mesh):
    return jax.shard_map(
        on_device,
        mesh=mesh,
        in_specs=(
            P(("dp", "seq"), None),
            P(("dp", "seq"), "head"),
            P(("dp", "seq"), "head"),
            P(("dp", "seq"), "head"),
            P(("dp", "seq"), "head"),
            P(("dp", "seq"), "head"),
            P(("dp", "seq"), "head"),
            P(("dp", "head"), None, None),
            P(),
            P("head", None),
            P(),
            P(("dp", "seq"), None),
            P(("dp", "seq"), None),
            P(("seq", "head"), None, None),
            P(("seq", "head"), None, None),
            P(("seq", "head"), None, None),
        ),
        out_specs=P(("dp", "seq"), "head"),
        check_vma=False,
    )
```

```python
import jax
import jax.numpy as jnp
from jax import lax
from jax.sharding import PartitionSpec as P

VALUE_HEAD_COUNT = 32
QK_HEADS = 16
DK = 128
DV = 128


precise_variant = lax.Precision.HIGHEST


def unit_rows(matrix):
    return matrix * lax.rsqrt(jnp.sum(matrix * matrix, axis=-1, keepdims=True) + 1e-06)


def batch_product(left, right):
    return jnp.einsum("hij,hjk->hik", left, right, precision=precise_variant)


def batch_product_wide(left, right_a, right_b):
    joined = jnp.einsum(
        "hij,hjk->hik",
        left,
        jnp.concatenate([right_a, right_b], axis=-1),
        precision=precise_variant,
    )
    return joined


def block_product(left, right):
    return jnp.einsum("...ij,...jk->...ik", left, right, precision=precise_variant)


def unit_lower_inverse(tri, block=16):
    heads, size_all, _ = tri.shape
    count = size_all // block
    eye_block = jnp.eye(block, dtype=tri.dtype)
    diagonal = jnp.stack(
        [tri[:, k * block : (k + 1) * block, k * block : (k + 1) * block] for k in range(count)],
        axis=1,
    )
    nil = diagonal - eye_block
    power = block_product(nil, nil)
    inverse = block_product(eye_block - nil, eye_block + power)
    reach = 4
    while reach < block:
        power = block_product(power, power)
        inverse = block_product(inverse, eye_block + power)
        reach *= 2
    size = block
    while size < size_all:
        pairs = inverse.shape[1] // 2
        first = inverse[:, 0::2]
        second = inverse[:, 1::2]
        coupling = jnp.stack(
            [
                tri[:, (2 * k + 1) * size : (2 * k + 2) * size, 2 * k * size : (2 * k + 1) * size]
                for k in range(pairs)
            ],
            axis=1,
        )
        lower_left = -block_product(second, block_product(coupling, first))
        top = jnp.concatenate([first, jnp.zeros_like(first)], axis=-1)
        bottom = jnp.concatenate([lower_left, second], axis=-1)
        inverse = jnp.concatenate([top, bottom], axis=-2)
        size *= 2
    return inverse[:, 0]


def on_device(
    stream,
    queries,
    keys,
    values,
    out_gate,
    gates,
    betas,
    init_state,
    norm_gain,
    out_proj,
    post_gain,
    expert_ids,
    route_scores,
    w_gate,
    w_up,
    w_down,
):
    length = stream.shape[0]
    model_width = stream.shape[1]
    head_count = values.shape[1] // DV
    group_size = VALUE_HEAD_COUNT // QK_HEADS
    scaled_q = unit_rows(queries.astype(jnp.float32).reshape(length, -1, DK)) * DK ** (-0.5)
    query_head_rows = jnp.repeat(scaled_q, group_size, axis=1).transpose(1, 0, 2)
    unit_k = unit_rows(keys.astype(jnp.float32).reshape(length, -1, DK))
    key_heads = jnp.repeat(unit_k, group_size, axis=1).transpose(1, 0, 2)
    value_heads = values.astype(jnp.float32).reshape(length, head_count, DV).transpose(1, 0, 2)
    beta_heads = betas.T
    log_decay = jnp.cumsum(jnp.log(gates), axis=0).T
    row_index = lax.broadcasted_iota(jnp.int32, (length, length), 0)
    col_index = lax.broadcasted_iota(jnp.int32, (length, length), 1)
    lower = row_index >= col_index
    strict = row_index > col_index
    gap_log = log_decay[:, :, None] - log_decay[:, None, :]
    decay = jnp.where(lower, jnp.exp(jnp.where(lower, gap_log, 0.0)), 0.0)
    key_inner = jnp.einsum("htk,hsk->hts", key_heads, key_heads, precision=precise_variant)
    tri_matrix = jnp.where(strict, decay * key_inner, 0.0) * beta_heads[:, :, None] + jnp.eye(
        length, dtype=jnp.float32
    )
    decay_factor = jnp.exp(log_decay)
    right_side = jnp.concatenate(
        [beta_heads[:, :, None] * value_heads, (beta_heads * decay_factor)[:, :, None] * key_heads],
        axis=-1,
    )
    solved = batch_product(unit_lower_inverse(tri_matrix), right_side)
    new_contribution = solved[:, :, :DV]
    carried_state = solved[:, :, DV:]
    tail_decay = jnp.exp(log_decay[:, -1:] - log_decay)
    keys_weighted = key_heads * tail_decay[:, :, None]
    eye_keys = jnp.eye(DK, dtype=jnp.float32)
    state_map = decay_factor[:, -1][:, None, None] * eye_keys - jnp.einsum(
        "htk,htj->hkj", keys_weighted, carried_state, precision=precise_variant
    )
    state_increment = jnp.einsum(
        "iys,iyn->isn", keys_weighted, new_contribution, precision=precise_variant
    )

    query_inner = (
        jnp.einsum("htk,hsk->hts", query_head_rows, key_heads, precision=precise_variant) * decay
    )
    query_effective = query_head_rows * decay_factor[:, :, None] - batch_product(
        query_inner, carried_state
    )
    core_local = batch_product(query_inner, new_contribution)
    own_pair = jnp.concatenate([state_map, state_increment], axis=0).astype(jnp.bfloat16)
    ring = lax.axis_size("seq")
    position = lax.axis_index("seq")
    forward_pairs = [(j, (j + 1) % ring) for j in range(ring)]
    backward_pairs = [(j, (j - 1) % ring) for j in range(ring)]
    going_up = own_pair
    going_down = own_pair
    later_map = None
    later_add = None
    opening_state = init_state
    for step in range(1, ring // 2 + 1):
        going_up = lax.ppermute(going_up, "seq", forward_pairs)
        piece = going_up.astype(jnp.float32)
        if later_map is None:
            later_map = piece[:head_count]
            later_add = piece[head_count:]
        else:
            joined = batch_product_wide(later_map, piece[:head_count], piece[head_count:])
            useful = step <= position
            later_add = jnp.where(useful, joined[..., DK:] + later_add, later_add)
            later_map = jnp.where(useful, joined[..., :DK], later_map)
        if step < ring - step:
            going_down = lax.ppermute(going_down, "seq", backward_pairs)
            piece = going_down.astype(jnp.float32)
            advanced = batch_product(piece[:head_count], opening_state) + piece[head_count:]
            opening_state = jnp.where(position + step >= ring, advanced, opening_state)
    carried_open = batch_product(later_map, opening_state) + later_add
    opening_state = jnp.where(position > 0, carried_open, opening_state)
    core = batch_product(query_effective, opening_state) + core_local
    core = core.transpose(1, 0, 2)
    gate_rows = out_gate.astype(jnp.float32).reshape(length, head_count, DV)
    gated = (
        core
        * lax.rsqrt(jnp.mean(core * core, axis=-1, keepdims=True) + 1e-06)
        * norm_gain
        * jax.nn.silu(gate_rows)
    )
    gated = gated.astype(jnp.bfloat16).reshape(length, head_count * DV)
    attn_part = jnp.dot(gated, out_proj, preferred_element_type=jnp.float32)
    share_width = model_width // lax.axis_size("head")
    share_start = lax.axis_index("head") * share_width
    column_total = lax.axis_size("head")
    attn_pieces = attn_part.astype(jnp.bfloat16).reshape(length, column_total, share_width)
    attn_pieces = lax.all_to_all(
        attn_pieces.transpose(1, 0, 2), "head", split_axis=0, concat_axis=0, tiled=True
    )
    attn_share = jnp.sum(attn_pieces.astype(jnp.float32), axis=0)
    stream_share = lax.dynamic_slice_in_dim(stream, share_start, share_width, 1)
    resid_share = (stream_share.astype(jnp.float32) + attn_share).astype(jnp.bfloat16)
    resid_share = lax.optimization_barrier(resid_share)
    resid_rows = lax.all_to_all(
        jnp.broadcast_to(resid_share[None], (column_total, length, share_width)),
        "head",
        split_axis=0,
        concat_axis=0,
        tiled=True,
    )
    resid = resid_rows.transpose(1, 0, 2).reshape(length, model_width)
    resid_f = resid.astype(jnp.float32)
    normed = (
        resid_f * lax.rsqrt(jnp.mean(resid_f * resid_f, axis=-1, keepdims=True) + 1e-06) * post_gain
    ).astype(jnp.bfloat16)
    peer_count = lax.axis_size("seq")
    column_count = lax.axis_size("head")
    expert_count = peer_count * column_count
    pick_count = expert_ids.shape[1]
    slot_count = min(length, length * pick_count * 2 // expert_count)
    targets = jnp.arange(peer_count, dtype=jnp.int32) * column_count + lax.axis_index("head")
    hits = expert_ids[:, :, None] == targets[None, None, :]
    weights = (route_scores / jnp.sum(route_scores, axis=1, keepdims=True)).astype(jnp.bfloat16)
    weights = lax.optimization_barrier(weights).astype(jnp.float32)
    chosen = jnp.sum(hits.astype(jnp.int32), axis=1)
    share_weight = jnp.sum(jnp.where(hits, weights[:, :, None], 0.0), axis=1)
    rank = jnp.cumsum(chosen, axis=0) - chosen
    slot_index = jnp.arange(slot_count, dtype=jnp.int32)
    placement_map = (
        (chosen[:, :, None] == 1) & (rank[:, :, None] == slot_index[None, None, :])
    ).astype(jnp.bfloat16)
    outgoing = jnp.einsum(
        "tps,td->psd", placement_map, normed, preferred_element_type=jnp.float32
    ).astype(jnp.bfloat16)
    incoming = lax.all_to_all(outgoing, "seq", split_axis=0, concat_axis=0, tiled=True)
    gate_e = jnp.einsum("psd,dh->psh", incoming, w_gate[0], preferred_element_type=jnp.float32)
    up_e = jnp.einsum("psd,dh->psh", incoming, w_up[0], preferred_element_type=jnp.float32)
    hidden = (jax.nn.silu(gate_e) * up_e).astype(jnp.bfloat16)
    down_pieces = w_down[0].reshape(w_down.shape[1], column_count, share_width)
    sliced = jnp.einsum(
        "psh,hcd->pcsd", hidden, down_pieces, preferred_element_type=jnp.float32
    ).astype(jnp.bfloat16)
    sliced = sliced.reshape(expert_count, slot_count, share_width)
    returned = lax.all_to_all(sliced, ("seq", "head"), split_axis=0, concat_axis=0, tiled=True)
    every_expert = jnp.arange(expert_count, dtype=jnp.int32)
    hits_all = expert_ids[:, :, None] == every_expert[None, None, :]
    chosen_all = jnp.sum(hits_all.astype(jnp.int32), axis=1)
    weight_all = jnp.sum(jnp.where(hits_all, weights[:, :, None], 0.0), axis=1)
    rank_all = jnp.cumsum(chosen_all, axis=0) - chosen_all
    combine_all = jnp.where(
        (chosen_all[:, :, None] == 1) & (rank_all[:, :, None] == slot_index[None, None, :]),
        weight_all[:, :, None],
        0.0,
    ).astype(jnp.bfloat16)
    moe_share = jnp.einsum(
        "tes,esc->tc", combine_all, returned, preferred_element_type=jnp.float32
    )
    return (resid_share.astype(jnp.float32) + moe_share).astype(jnp.bfloat16)


def solution(mesh):
    return jax.shard_map(
        on_device,
        mesh=mesh,
        in_specs=(
            P(("dp", "seq"), None),
            P(("dp", "seq"), "head"),
            P(("dp", "seq"), "head"),
            P(("dp", "seq"), "head"),
            P(("dp", "seq"), "head"),
            P(("dp", "seq"), "head"),
            P(("dp", "seq"), "head"),
            P(("dp", "head"), None, None),
            P(),
            P("head", None),
            P(),
            P(("dp", "seq"), None),
            P(("dp", "seq"), None),
            P(("seq", "head"), None, None),
            P(("seq", "head"), None, None),
            P(("seq", "head"), None, None),
        ),
        out_specs=P(("dp", "seq"), "head"),
        check_vma=False,
    )
```

```python
import jax
import jax.numpy as jnp
from jax import lax
from jax.sharding import PartitionSpec as P

VALUE_HEAD_COUNT = 32
QK_HEADS = 16
DK = 128
DV = 128


precise_variant = lax.Precision.HIGHEST


def unit_rows(matrix):
    return matrix * lax.rsqrt(jnp.sum(matrix * matrix, axis=-1, keepdims=True) + 1e-06)


def batch_product(left, right):
    return jnp.einsum("hij,hjk->hik", left, right, precision=precise_variant)


def batch_product_wide(left, right_a, right_b):
    joined = jnp.einsum(
        "hij,hjk->hik",
        left,
        jnp.concatenate([right_a, right_b], axis=-1),
        precision=precise_variant,
    )
    return joined


def block_product(left, right):
    return jnp.einsum("...ij,...jk->...ik", left, right, precision=precise_variant)


def unit_lower_inverse(tri, block=16):
    heads, size_all, _ = tri.shape
    count = size_all // block
    eye_block = jnp.eye(block, dtype=tri.dtype)
    diagonal = jnp.stack(
        [tri[:, k * block : (k + 1) * block, k * block : (k + 1) * block] for k in range(count)],
        axis=1,
    )
    nil = diagonal - eye_block
    power = block_product(nil, nil)
    inverse = block_product(eye_block - nil, eye_block + power)
    reach = 4
    while reach < block:
        power = block_product(power, power)
        inverse = block_product(inverse, eye_block + power)
        reach *= 2
    size = block
    while size < size_all:
        pairs = inverse.shape[1] // 2
        first = inverse[:, 0::2]
        second = inverse[:, 1::2]
        coupling = jnp.stack(
            [
                tri[:, (2 * k + 1) * size : (2 * k + 2) * size, 2 * k * size : (2 * k + 1) * size]
                for k in range(pairs)
            ],
            axis=1,
        )
        lower_left = -block_product(second, block_product(coupling, first))
        top = jnp.concatenate([first, jnp.zeros_like(first)], axis=-1)
        bottom = jnp.concatenate([lower_left, second], axis=-1)
        inverse = jnp.concatenate([top, bottom], axis=-2)
        size *= 2
    return inverse[:, 0]


def on_device(
    stream,
    queries,
    keys,
    values,
    out_gate,
    gates,
    betas,
    init_state,
    norm_gain,
    out_proj,
    post_gain,
    expert_ids,
    route_scores,
    w_gate,
    w_up,
    w_down,
):
    length = stream.shape[0]
    model_width = stream.shape[1]
    head_count = values.shape[1] // DV
    group_size = VALUE_HEAD_COUNT // QK_HEADS
    scaled_q = unit_rows(queries.astype(jnp.float32).reshape(length, -1, DK)) * DK ** (-0.5)
    query_head_rows = jnp.repeat(scaled_q, group_size, axis=1).transpose(1, 0, 2)
    unit_k = unit_rows(keys.astype(jnp.float32).reshape(length, -1, DK))
    key_heads = jnp.repeat(unit_k, group_size, axis=1).transpose(1, 0, 2)
    value_heads = values.astype(jnp.float32).reshape(length, head_count, DV).transpose(1, 0, 2)
    beta_heads = betas.T
    log_decay = jnp.cumsum(jnp.log(gates), axis=0).T
    row_index = lax.broadcasted_iota(jnp.int32, (length, length), 0)
    col_index = lax.broadcasted_iota(jnp.int32, (length, length), 1)
    lower = row_index >= col_index
    strict = row_index > col_index
    gap_log = log_decay[:, :, None] - log_decay[:, None, :]
    decay = jnp.where(lower, jnp.exp(jnp.where(lower, gap_log, 0.0)), 0.0)
    key_inner = jnp.einsum("htk,hsk->hts", key_heads, key_heads, precision=precise_variant)
    tri_matrix = jnp.where(strict, decay * key_inner, 0.0) * beta_heads[:, :, None] + jnp.eye(
        length, dtype=jnp.float32
    )
    decay_factor = jnp.exp(log_decay)
    right_side = jnp.concatenate(
        [beta_heads[:, :, None] * value_heads, (beta_heads * decay_factor)[:, :, None] * key_heads],
        axis=-1,
    )
    solved = batch_product(unit_lower_inverse(tri_matrix), right_side)
    new_contribution = solved[:, :, :DV]
    carried_state = solved[:, :, DV:]
    tail_decay = jnp.exp(log_decay[:, -1:] - log_decay)
    keys_weighted = key_heads * tail_decay[:, :, None]
    eye_keys = jnp.eye(DK, dtype=jnp.float32)
    state_map = decay_factor[:, -1][:, None, None] * eye_keys - jnp.einsum(
        "htk,htj->hkj", keys_weighted, carried_state, precision=precise_variant
    )
    state_increment = jnp.einsum(
        "iys,iyn->isn", keys_weighted, new_contribution, precision=precise_variant
    )

    query_inner = (
        jnp.einsum("htk,hsk->hts", query_head_rows, key_heads, precision=precise_variant) * decay
    )
    query_effective = query_head_rows * decay_factor[:, :, None] - batch_product(
        query_inner, carried_state
    )
    core_local = batch_product(query_inner, new_contribution)
    own_pair = jnp.concatenate([state_map, state_increment], axis=0).astype(jnp.bfloat16)
    ring = lax.axis_size("seq")
    position = lax.axis_index("seq")
    forward_pairs = [(j, (j + 1) % ring) for j in range(ring)]
    backward_pairs = [(j, (j - 1) % ring) for j in range(ring)]
    going_up = own_pair
    going_down = own_pair
    later_map = None
    later_add = None
    opening_state = init_state
    for step in range(1, ring // 2 + 1):
        going_up = lax.ppermute(going_up, "seq", forward_pairs)
        piece = going_up.astype(jnp.float32)
        if later_map is None:
            later_map = piece[:head_count]
            later_add = piece[head_count:]
        else:
            joined = batch_product_wide(later_map, piece[:head_count], piece[head_count:])
            useful = step <= position
            later_add = jnp.where(useful, joined[..., DK:] + later_add, later_add)
            later_map = jnp.where(useful, joined[..., :DK], later_map)
        if step < ring - step:
            going_down = lax.ppermute(going_down, "seq", backward_pairs)
            piece = going_down.astype(jnp.float32)
            advanced = batch_product(piece[:head_count], opening_state) + piece[head_count:]
            opening_state = jnp.where(position + step >= ring, advanced, opening_state)
    carried_open = batch_product(later_map, opening_state) + later_add
    opening_state = jnp.where(position > 0, carried_open, opening_state)
    core = batch_product(query_effective, opening_state) + core_local
    core = core.transpose(1, 0, 2)
    gate_rows = out_gate.astype(jnp.float32).reshape(length, head_count, DV)
    gated = (
        core
        * lax.rsqrt(jnp.mean(core * core, axis=-1, keepdims=True) + 1e-06)
        * norm_gain
        * jax.nn.silu(gate_rows)
    )
    gated = gated.astype(jnp.bfloat16).reshape(length, head_count * DV)
    share_width = model_width // lax.axis_size("head")
    share_start = lax.axis_index("head") * share_width
    column_total = lax.axis_size("head")
    attn_pieces = jnp.einsum(
        "tk,kcd->ctd",
        gated,
        out_proj.reshape(out_proj.shape[0], column_total, share_width),
        preferred_element_type=jnp.float32,
    ).astype(jnp.bfloat16)
    attn_pieces = lax.all_to_all(attn_pieces, "head", split_axis=0, concat_axis=0, tiled=True)
    attn_share = jnp.sum(attn_pieces.astype(jnp.float32), axis=0)
    stream_share = lax.dynamic_slice_in_dim(stream, share_start, share_width, 1)
    resid_share = (stream_share.astype(jnp.float32) + attn_share).astype(jnp.bfloat16)
    resid_share = lax.optimization_barrier(resid_share)
    resid_rows = lax.all_to_all(
        jnp.broadcast_to(resid_share[None], (column_total, length, share_width)),
        "head",
        split_axis=0,
        concat_axis=0,
        tiled=True,
    )
    resid = resid_rows.transpose(1, 0, 2).reshape(length, model_width)
    resid_f = resid.astype(jnp.float32)
    normed = (
        resid_f * lax.rsqrt(jnp.mean(resid_f * resid_f, axis=-1, keepdims=True) + 1e-06) * post_gain
    ).astype(jnp.bfloat16)
    peer_count = lax.axis_size("seq")
    column_count = lax.axis_size("head")
    expert_count = peer_count * column_count
    pick_count = expert_ids.shape[1]
    slot_count = min(length, length * pick_count * 2 // expert_count)
    targets = jnp.arange(peer_count, dtype=jnp.int32) * column_count + lax.axis_index("head")
    hits = expert_ids[:, :, None] == targets[None, None, :]
    weights = (route_scores / jnp.sum(route_scores, axis=1, keepdims=True)).astype(jnp.bfloat16)
    weights = lax.optimization_barrier(weights).astype(jnp.float32)
    chosen = jnp.sum(hits.astype(jnp.int32), axis=1)
    share_weight = jnp.sum(jnp.where(hits, weights[:, :, None], 0.0), axis=1)
    rank = jnp.cumsum(chosen, axis=0) - chosen
    slot_index = jnp.arange(slot_count, dtype=jnp.int32)
    placement_map = (
        (chosen[:, :, None] == 1) & (rank[:, :, None] == slot_index[None, None, :])
    ).astype(jnp.bfloat16)
    outgoing = jnp.einsum(
        "tps,td->psd", placement_map, normed, preferred_element_type=jnp.float32
    ).astype(jnp.bfloat16)
    incoming = lax.all_to_all(outgoing, "seq", split_axis=0, concat_axis=0, tiled=True)
    gate_e = jnp.einsum("psd,dh->psh", incoming, w_gate[0], preferred_element_type=jnp.float32)
    up_e = jnp.einsum("psd,dh->psh", incoming, w_up[0], preferred_element_type=jnp.float32)
    hidden = (jax.nn.silu(gate_e) * up_e).astype(jnp.bfloat16)
    down_pieces = w_down[0].reshape(w_down.shape[1], column_count, share_width)
    sliced = jnp.einsum(
        "psh,hcd->pcsd", hidden, down_pieces, preferred_element_type=jnp.float32
    ).astype(jnp.bfloat16)
    sliced = sliced.reshape(expert_count, slot_count, share_width)
    returned = lax.all_to_all(sliced, ("seq", "head"), split_axis=0, concat_axis=0, tiled=True)
    every_expert = jnp.arange(expert_count, dtype=jnp.int32)
    hits_all = expert_ids[:, :, None] == every_expert[None, None, :]
    chosen_all = jnp.sum(hits_all.astype(jnp.int32), axis=1)
    weight_all = jnp.sum(jnp.where(hits_all, weights[:, :, None], 0.0), axis=1)
    rank_all = jnp.cumsum(chosen_all, axis=0) - chosen_all
    combine_all = jnp.where(
        (chosen_all[:, :, None] == 1) & (rank_all[:, :, None] == slot_index[None, None, :]),
        weight_all[:, :, None],
        0.0,
    ).astype(jnp.bfloat16)
    moe_share = jnp.einsum(
        "tes,esc->tc", combine_all, returned, preferred_element_type=jnp.float32
    )
    return (resid_share.astype(jnp.float32) + moe_share).astype(jnp.bfloat16)


def solution(mesh):
    return jax.shard_map(
        on_device,
        mesh=mesh,
        in_specs=(
            P(("dp", "seq"), None),
            P(("dp", "seq"), "head"),
            P(("dp", "seq"), "head"),
            P(("dp", "seq"), "head"),
            P(("dp", "seq"), "head"),
            P(("dp", "seq"), "head"),
            P(("dp", "seq"), "head"),
            P(("dp", "head"), None, None),
            P(),
            P("head", None),
            P(),
            P(("dp", "seq"), None),
            P(("dp", "seq"), None),
            P(("seq", "head"), None, None),
            P(("seq", "head"), None, None),
            P(("seq", "head"), None, None),
        ),
        out_specs=P(("dp", "seq"), "head"),
        check_vma=False,
    )
```
